128 devices in a mesh: cfg: 2 (over core), orbit: 32 (over z, x_lo, y), tp: 2 (over x_hi).
Axes of the slice: x: 4 (x_hi: 2, x_lo: 2; x = x_hi * 2 + x_lo), y: 4, z: 4, core: 2. Of those that a mesh axis runs over, the one named last changes fastest.
Arguments:
- tokens: bfloat16 [2, 32, 1024, 1536], P('cfg', 'orbit', 'tp'), may hold values from -6 to 6
- modulation: float32 [2, 2, 1536], P('cfg'), may hold values from -2 to 6
- w_qkv: bfloat16 [1536, 3, 1536], P(None, None, 'tp'), may hold values from -1 to 1
- w_out: bfloat16 [1536, 1536], P('tp'), may hold values from -0.15625 to 0.15625
- adjacency: int32 [32, 4, 8], P('orbit'), may hold values 0 or 1
Outputs:
- guided: bfloat16 [32, 1024, 1536], P('orbit', 'tp', 'cfg')
The draws below stay inside these ranges and needn't reach their ends.
All inputs are finite; a program needn't handle non-finite values. No bound on the sum of `adjacency` on one device may be relied on, other than what follows from the above.
Results may differ from the reference program's by a relative error of at most 0.0075.
Values may be sent and summed in bfloat16 or wider, within the bound.
No kernel may reach another device: no remote copies, remote signals or barrier semaphores. Data moves between devices by JAX's collectives and lax.ppermute only.
A program may use at most 128 MiB of HBM per device.

```python
import jax
import jax.numpy as jnp
from jax import lax

D = 1536
HEAD_DIM = 128
HEADS = 12
TOK_VIEW = 1024
BLOCK = 128
KEY_BLOCKS = 8
REACH = 2
VIEWS = 32


def draw_modulation(key, part):
    first = jax.random.fold_in(jax.random.fold_in(key, 11), 0)
    base = jnp.clip(jax.random.normal(first, (2, 2, D), jnp.float32) * 0.5, -2.0, 2.0)
    return base


def draw_w_qkv(key, part):
    first = jax.random.fold_in(jax.random.fold_in(key, 23), 0)
    spread = D ** (-0.5)
    return (jnp.clip(jax.random.normal(first, (D, 3, D), jnp.float32), -5.0, 5.0) * spread).astype(jnp.bfloat16)


def set_ends(drawn, stream_key, low, largest):
    extent = drawn.shape
    spot = [jax.random.randint(jax.random.fold_in(stream_key, axis), (), 0, extent[axis]) for axis in range(len(extent))]
    drawn = drawn.at[tuple(spot)].set(low)
    longest = extent.index(max(extent))
    spot[longest] = (spot[longest] + 1) % extent[longest]
    return drawn.at[tuple(spot)].set(largest)


def levels(key, dims, pieces, smallest, top_value):
    def one(axis_at, shards_of):
        steps = jax.random.uniform(jax.random.fold_in(jax.random.fold_in(key, 6), axis_at), (shards_of,), jnp.float32, smallest / len(pieces), top_value / len(pieces))
        return jnp.repeat(jnp.exp(steps), dims[axis_at] // shards_of).reshape((-1,) + (1,) * (len(dims) - axis_at - 1))

    gain = one(*pieces[0])
    for cut in pieces[1:]:
        gain = gain * one(*cut)
    return gain


def normal_values(stream_key, shape, scale, most, pieces=(), held_as=jnp.bfloat16):
    values = jax.random.normal(stream_key, shape, jnp.float32) * scale
    if len(pieces) > 0:
        values = levels(stream_key, shape, pieces, -0.22, 0.18) * values
    return jnp.clip(values, min=-most, max=most).astype(held_as)


def setup_inputs(seed: int = 0) -> dict:
    seeds = jax.random.split(jax.random.key(seed), 6)
    tokens = normal_values(seeds[0], (2, VIEWS, TOK_VIEW, D), 1.0, 6.0, ((0, 2), (1, 32), (2, 2)))
    modulation = draw_modulation(jax.random.fold_in(seeds[5], 71), 0)
    w_qkv = draw_w_qkv(jax.random.fold_in(seeds[5], 71), 0)
    w_out = normal_values(seeds[3], (D, D), D ** -0.5, 0.15625, ((0, 2),))
    adjacency = set_ends((jax.random.randint(seeds[4], (VIEWS, 2 * REACH, KEY_BLOCKS), 0, 4) < 3).astype(jnp.int32), jax.random.fold_in(seeds[4], 1), 0, 1)
    return {"tokens": tokens, "modulation": modulation, "w_qkv": w_qkv, "w_out": w_out, "adjacency": adjacency}


guide_scale = 4.0

def attend_head(queries, keyset, valueset, keymask):
    scores = jnp.dot(queries, keyset.T, preferred_element_type=jnp.float32) * queries.shape[1] ** (-0.5)
    scores = jnp.where(keymask[None, :], scores, -1e+30)
    peak = lax.optimization_barrier(jnp.max(scores, axis=1, keepdims=True))
    expon = jnp.exp(scores - peak)
    total = lax.optimization_barrier(jnp.sum(expon, axis=1, keepdims=True))
    weights = expon.astype(jnp.bfloat16)
    return (jnp.dot(weights, valueset, preferred_element_type=jnp.float32) / total).astype(jnp.bfloat16)

def reference(tokens, modulation, w_qkv, w_out, adjacency):
    flat_weight = w_qkv.reshape(D, 3 * D)

    def project(index):
        branch = index // VIEWS
        view = index % VIEWS
        inputs = tokens[branch, view].astype(jnp.float32)
        squares = lax.optimization_barrier(jnp.mean(inputs * inputs, axis=1, keepdims=True))
        shift_scale = modulation[branch]
        normed = (inputs * lax.rsqrt(squares + 1e-06) * (1.0 + shift_scale[1]) + shift_scale[0]).astype(jnp.bfloat16)
        return jnp.dot(normed, flat_weight, preferred_element_type=jnp.float32).astype(jnp.bfloat16).reshape(TOK_VIEW, 3, D)
    qkv_all = lax.map(project, jnp.arange(2 * VIEWS, dtype=jnp.int32))
    offsets = jnp.arange(-REACH, REACH + 1, dtype=jnp.int32)

    def attend_view(index):
        branch = index // VIEWS
        view = index % VIEWS
        queries = qkv_all[index, :, 0]
        neighbours = (view + offsets + VIEWS) % VIEWS
        gathered = qkv_all[branch * VIEWS + neighbours]
        keyflat = gathered[:, :, 1].reshape((2 * REACH + 1) * TOK_VIEW, D)
        valflat = gathered[:, :, 2].reshape((2 * REACH + 1) * TOK_VIEW, D)
        flags = adjacency[view]
        allowed = jnp.concatenate([flags[:REACH], jnp.ones((1, KEY_BLOCKS), jnp.int32), flags[REACH:]], axis=0)
        keymask = jnp.repeat(allowed, BLOCK, axis=1).reshape(-1) > 0

        def one_head(head_index):
            start = head_index * HEAD_DIM
            return attend_head(lax.dynamic_slice_in_dim(queries, start, HEAD_DIM, 1), lax.dynamic_slice_in_dim(keyflat, start, HEAD_DIM, 1), lax.dynamic_slice_in_dim(valflat, start, HEAD_DIM, 1), keymask)
        heads_out = lax.map(one_head, jnp.arange(HEADS, dtype=jnp.int32))
        context = jnp.transpose(heads_out, (1, 0, 2)).reshape(TOK_VIEW, D)
        return jnp.dot(context, w_out, preferred_element_type=jnp.float32).astype(jnp.bfloat16)
    branch_out = lax.map(attend_view, jnp.arange(2 * VIEWS, dtype=jnp.int32)).reshape(2, VIEWS, TOK_VIEW, D)
    guided = (1.0 - guide_scale) * branch_out[1].astype(jnp.float32) + guide_scale * branch_out[0].astype(jnp.float32)
    return guided.astype(jnp.bfloat16)
```

```python
import jax
import jax.numpy as jnp
from jax import lax
from jax.sharding import PartitionSpec as P

HEAD_DIM = 128
REACH = 2


guide_scale = 4.0


def from_behind(array, axis, by):
    count = lax.axis_size(axis)
    return lax.ppermute(array, axis, [(i, (i + by) % count) for i in range(count)])


def attend_head(queries, keyset, valueset, keymask):
    scores = jnp.dot(queries, keyset.T, preferred_element_type=jnp.float32) * queries.shape[1] ** (
        -0.5
    )
    scores = jnp.where(keymask[None, :], scores, -1e30)
    peak = jnp.max(scores, axis=1, keepdims=True)
    expon = jnp.exp(scores - peak)
    total = jnp.sum(expon, axis=1, keepdims=True)
    weights = expon.astype(jnp.bfloat16)
    return (jnp.dot(weights, valueset, preferred_element_type=jnp.float32) / total).astype(
        jnp.bfloat16
    )


def direct_send(payload, amount):
    return from_behind(payload, "orbit", amount)


def per_device(tokens, modulation, w_qkv, w_out, adjacency):
    inputs = tokens[0, 0].astype(jnp.float32)
    width = inputs.shape[1]
    half_heads = w_qkv.shape[2]
    shift_scale = modulation[0]
    squares = jnp.mean(inputs * inputs, axis=1, keepdims=True)
    normed = (inputs * lax.rsqrt(squares + 1e-06) * (1.0 + shift_scale[1]) + shift_scale[0]).astype(
        jnp.bfloat16
    )
    whole = lax.all_gather(normed, "tp", axis=0, tiled=True)
    rows_view = whole.shape[0]
    qkv = jnp.dot(whole, w_qkv.reshape(width, 3 * half_heads), preferred_element_type=jnp.float32)
    qkv = qkv.astype(jnp.bfloat16).reshape(rows_view, 3, half_heads)
    queries = qkv[:, 0]
    own_pair = qkv[:, 1:]
    chunks = 2
    pieces = jnp.split(own_pair, chunks, axis=2)
    received = {}
    for sign in (1, -1):
        near = [direct_send(piece, -sign) for piece in pieces]
        far = [direct_send(piece, -sign) for piece in near]
        received[sign] = jnp.concatenate(near, axis=2)
        received[2 * sign] = jnp.concatenate(far, axis=2)
    received[0] = own_pair
    stacked = jnp.stack([received[offset] for offset in range(-REACH, REACH + 1)], axis=0)
    keyflat = stacked[:, :, 0].reshape((2 * REACH + 1) * rows_view, half_heads)
    valflat = stacked[:, :, 1].reshape((2 * REACH + 1) * rows_view, half_heads)
    flags = adjacency[0]
    blocks = flags.shape[1]
    allowed = jnp.concatenate(
        [flags[:REACH], jnp.ones((1, blocks), jnp.int32), flags[REACH:]], axis=0
    )
    keymask = jnp.repeat(allowed, rows_view // blocks, axis=1).reshape(-1) > 0

    def one_head(head_index):
        start = head_index * HEAD_DIM
        return attend_head(
            lax.dynamic_slice_in_dim(queries, start, HEAD_DIM, 1),
            lax.dynamic_slice_in_dim(keyflat, start, HEAD_DIM, 1),
            lax.dynamic_slice_in_dim(valflat, start, HEAD_DIM, 1),
            keymask,
        )

    heads_out = lax.map(one_head, jnp.arange(half_heads // HEAD_DIM, dtype=jnp.int32))
    context = jnp.transpose(heads_out, (1, 0, 2)).reshape(rows_view, half_heads)
    partial = jnp.dot(context, w_out, preferred_element_type=jnp.float32)
    owner = lax.axis_index("cfg")
    weight_now = jnp.where(owner == 0, guide_scale, 1.0 - guide_scale).astype(jnp.float32)
    by_columns = lax.psum_scatter(weight_now * partial, "cfg", scatter_dimension=1, tiled=True)
    guided = lax.psum_scatter(by_columns, "tp", scatter_dimension=0, tiled=True)
    return guided.astype(jnp.bfloat16)[None]


def solution(mesh):
    return jax.shard_map(
        per_device,
        mesh=mesh,
        in_specs=(
            P("cfg", "orbit", "tp", None),
            P("cfg", None, None),
            P(None, None, "tp"),
            P("tp", None),
            P("orbit", None, None),
        ),
        out_specs=P("orbit", "tp", "cfg"),
        check_vma=False,
    )
```

```python
import functools

import jax
import jax.numpy as jnp
from jax import lax
from jax.experimental import pallas as pl
from jax.experimental.pallas import tpu as pltpu
from jax.sharding import PartitionSpec as P

HEAD_DIM = 128
REACH = 2
BLOCK = 128


guide_scale = 4.0


def from_behind(array, axis, by):
    count = lax.axis_size(axis)
    return lax.ppermute(array, axis, [(i, (i + by) % count) for i in range(count)])


def swap(array, axis):
    return lax.ppermute(array, axis, [(0, 1), (1, 0)])


def stage_kernel(*refs, n_chunks, first, last, masked, scale):
    flags_ref = refs[0]
    q_ref = refs[1]
    chunk_refs = refs[2 : 2 + 2 * n_chunks]
    rest = refs[2 + 2 * n_chunks :]
    if first:
        outs = rest
    else:
        m_in, l_in, acc_in = rest[:3]
        outs = rest[3:]
    q = q_ref[...]
    rows = q.shape[0]
    if first:
        m = jnp.full((rows, 1), -jnp.inf, jnp.float32)
        l = jnp.zeros((rows, 1), jnp.float32)
        acc = jnp.zeros((rows, HEAD_DIM), jnp.float32)
    else:
        m = m_in[:, :1]
        l = l_in[:, :1]
        acc = acc_in[...]
    for index in range(n_chunks):
        keys = chunk_refs[2 * index][...]
        values = chunk_refs[2 * index + 1][...]
        scores = lax.dot_general(
            q, keys, (((1,), (1,)), ((), ())), preferred_element_type=jnp.float32
        ) * scale
        if masked:
            width = keys.shape[0]
            column_block = lax.broadcasted_iota(jnp.int32, (1, width), 1) // BLOCK
            allowed = jnp.zeros((1, width), jnp.int32)
            for block in range(width // BLOCK):
                allowed = jnp.where(
                    column_block == block, flags_ref[index * (width // BLOCK) + block], allowed
                )
            scores = jnp.where(allowed > 0, scores, -1e30)
        m_new = jnp.maximum(m, jnp.max(scores, axis=1, keepdims=True))
        alpha = jnp.exp(m - m_new)
        expon = jnp.exp(scores - m_new)
        l = alpha * l + jnp.sum(expon, axis=1, keepdims=True)
        acc = alpha * acc + jnp.dot(
            expon.astype(jnp.bfloat16), values, preferred_element_type=jnp.float32
        )
        m = m_new
    if last:
        outs[0][...] = (acc / l).astype(outs[0].dtype)
    else:
        outs[0][...] = jnp.broadcast_to(m, outs[0].shape)
        outs[1][...] = jnp.broadcast_to(l, outs[1].shape)
        outs[2][...] = acc


def attend_stage(flags, queries, chunks, carry, *, first, last, masked, heads):
    rows = queries.shape[0]
    n_chunks = len(chunks)
    kernel = functools.partial(
        stage_kernel,
        n_chunks=n_chunks,
        first=first,
        last=last,
        masked=masked,
        scale=HEAD_DIM ** (-0.5),
    )
    q_spec = pl.BlockSpec((rows, HEAD_DIM), lambda h, f: (0, h))
    in_specs = [q_spec]
    operands = [queries]
    for chunk in chunks:
        width = chunk.shape[0]
        in_specs.append(pl.BlockSpec((width, HEAD_DIM), lambda h, f: (0, h)))
        in_specs.append(pl.BlockSpec((width, HEAD_DIM), lambda h, f: (0, heads + h)))
        operands += [chunk, chunk]
    carry_spec = pl.BlockSpec((rows, HEAD_DIM), lambda h, f: (0, h))
    if not first:
        in_specs += [carry_spec] * 3
        operands += list(carry)
    if last:
        out_shape = jax.ShapeDtypeStruct((rows, heads * HEAD_DIM), jnp.bfloat16)
        out_specs = carry_spec
    else:
        out_shape = [jax.ShapeDtypeStruct((rows, heads * HEAD_DIM), jnp.float32)] * 3
        out_specs = [carry_spec] * 3
    return pl.pallas_call(
        kernel,
        out_shape=out_shape,
        grid_spec=pltpu.PrefetchScalarGridSpec(
            num_scalar_prefetch=1,
            grid=(heads,),
            in_specs=in_specs,
            out_specs=out_specs,
        ),
        compiler_params=pltpu.CompilerParams(dimension_semantics=("arbitrary",)),
    )(flags, *operands)


def per_device(tokens, modulation, w_qkv, w_out, adjacency):
    inputs = tokens[0, 0].astype(jnp.float32)
    width = inputs.shape[1]
    half_heads = w_qkv.shape[2]
    heads = half_heads // HEAD_DIM
    shift_scale = modulation[0]
    squares = jnp.mean(inputs * inputs, axis=1, keepdims=True)
    normed = (inputs * lax.rsqrt(squares + 1e-06) * (1.0 + shift_scale[1]) + shift_scale[0]).astype(
        jnp.bfloat16
    )
    half_rows = normed.shape[0]
    partner_normed = swap(normed, "tp")
    flat_w = w_qkv.reshape(width, 3 * half_heads)
    qkv_own = jnp.dot(normed, flat_w, preferred_element_type=jnp.float32).astype(jnp.bfloat16)
    pair_own = qkv_own[:, half_heads:]
    qkv_other = jnp.dot(partner_normed, flat_w, preferred_element_type=jnp.float32).astype(
        jnp.bfloat16
    )
    pair_other = qkv_other[:, half_heads:]
    queries = jnp.concatenate([qkv_own[:, :half_heads], qkv_other[:, :half_heads]], axis=0)

    received = {}
    for sign in (1, -1):
        near = [from_behind(piece, "orbit", -sign) for piece in (pair_own, pair_other)]
        far = [from_behind(piece, "orbit", -sign) for piece in near]
        received[sign] = near
        received[2 * sign] = far

    tp_index = lax.axis_index("tp")
    flags = adjacency[0]
    blocks = flags.shape[1]
    per_chunk = blocks // 2
    own_start = tp_index * per_chunk
    other_start = (1 - tp_index) * per_chunk

    def chunk_flags(offsets):
        rows_of = []
        for offset in offsets:
            row = flags[offset + REACH if offset < 0 else offset + REACH - 1]
            rows_of.append(lax.dynamic_slice_in_dim(row, own_start, per_chunk))
            rows_of.append(lax.dynamic_slice_in_dim(row, other_start, per_chunk))
        return jnp.concatenate(rows_of).astype(jnp.int32)

    no_flags = jnp.ones((2 * per_chunk,), jnp.int32)
    carry = attend_stage(
        no_flags, queries, [pair_own, pair_other], None,
        first=True, last=False, masked=False, heads=heads,
    )
    carry = attend_stage(
        chunk_flags((-1, 1)), queries, received[-1] + received[1], carry,
        first=False, last=False, masked=True, heads=heads,
    )
    context = attend_stage(
        chunk_flags((-2, 2)), queries, received[-2] + received[2], carry,
        first=False, last=True, masked=True, heads=heads,
    )

    owner = lax.axis_index("cfg")
    half_width = width // 2
    weight_now = jnp.where(owner == 0, guide_scale, 1.0 - guide_scale).astype(jnp.float32)
    w_mine = lax.dynamic_slice_in_dim(w_out, owner * half_width, half_width, 1)
    w_theirs = lax.dynamic_slice_in_dim(w_out, (1 - owner) * half_width, half_width, 1)
    theirs = weight_now * jnp.dot(context, w_theirs, preferred_element_type=jnp.float32)
    mine = weight_now * jnp.dot(context, w_mine, preferred_element_type=jnp.float32)
    mine = mine + swap(theirs, "cfg")
    guided = mine[:half_rows] + swap(mine[half_rows:], "tp")
    return guided.astype(jnp.bfloat16)[None]


def solution(mesh):
    return jax.shard_map(
        per_device,
        mesh=mesh,
        in_specs=(
            P("cfg", "orbit", "tp", None),
            P("cfg", None, None),
            P(None, None, "tp"),
            P("tp", None),
            P("orbit", None, None),
        ),
        out_specs=P("orbit", "tp", "cfg"),
        check_vma=False,
    )
```

```python
import functools

import jax
import jax.numpy as jnp
from jax import lax
from jax.experimental import pallas as pl
from jax.experimental.pallas import tpu as pltpu
from jax.sharding import PartitionSpec as P

HEAD_DIM = 128
REACH = 2
BLOCK = 128


guide_scale = 4.0


def from_behind(array, axis, by):
    count = lax.axis_size(axis)
    return lax.ppermute(array, axis, [(i, (i + by) % count) for i in range(count)])


def swap(array, axis):
    return lax.ppermute(array, axis, [(0, 1), (1, 0)])


def stage_kernel(*refs, n_chunks, first, last, masked, scale):
    refs = list(refs)
    bias_ref = refs.pop(0) if masked else None
    q_ref = refs.pop(0)
    chunk_refs = refs[: 2 * n_chunks]
    rest = refs[2 * n_chunks :]
    if first:
        outs = rest
    else:
        m_in, l_in, acc_in = rest[:3]
        outs = rest[3:]
    q = q_ref[...]
    rows = q.shape[0]
    if first:
        m = jnp.full((rows, 1), -jnp.inf, jnp.float32)
        l = jnp.zeros((rows, 1), jnp.float32)
        acc = jnp.zeros((rows, HEAD_DIM), jnp.float32)
    else:
        m = m_in[:, :1]
        l = l_in[:, :1]
        acc = acc_in[...]
    for index in range(n_chunks):
        keys = chunk_refs[2 * index][...]
        values = chunk_refs[2 * index + 1][...]
        width = keys.shape[0]
        scores = lax.dot_general(
            q, keys, (((1,), (1,)), ((), ())), preferred_element_type=jnp.float32
        ) * scale
        if masked:
            scores = scores + bias_ref[:, index * width : (index + 1) * width]
        m_new = jnp.maximum(m, jnp.max(scores, axis=1, keepdims=True))
        alpha = jnp.exp(m - m_new)
        expon = jnp.exp(scores - m_new)
        l = alpha * l + jnp.sum(expon, axis=1, keepdims=True)
        acc = alpha * acc + jnp.dot(
            expon.astype(jnp.bfloat16), values, preferred_element_type=jnp.float32
        )
        m = m_new
    if last:
        outs[0][...] = (acc / l).astype(outs[0].dtype)
    else:
        outs[0][...] = jnp.broadcast_to(m, outs[0].shape)
        outs[1][...] = jnp.broadcast_to(l, outs[1].shape)
        outs[2][...] = acc


def attend_stage(queries, chunks, bias, carry, *, first, last, heads, row_block=0, rows=None):
    rows = queries.shape[0] if rows is None else rows
    n_chunks = len(chunks)
    masked = bias is not None
    kernel = functools.partial(
        stage_kernel,
        n_chunks=n_chunks,
        first=first,
        last=last,
        masked=masked,
        scale=HEAD_DIM ** (-0.5),
    )
    row_spec = pl.BlockSpec((rows, HEAD_DIM), lambda h: (row_block, h))
    in_specs = []
    operands = []
    if masked:
        in_specs.append(pl.BlockSpec(bias.shape, lambda h: (0, 0)))
        operands.append(bias)
    in_specs.append(row_spec)
    operands.append(queries)
    for chunk in chunks:
        width = chunk.shape[0]
        in_specs.append(pl.BlockSpec((width, HEAD_DIM), lambda h: (0, h)))
        in_specs.append(pl.BlockSpec((width, HEAD_DIM), lambda h: (0, heads + h)))
        operands += [chunk, chunk]
    if not first:
        in_specs += [row_spec] * 3
        operands += list(carry)
    out_spec = pl.BlockSpec((rows, HEAD_DIM), lambda h: (0, h))
    if last:
        out_shape = jax.ShapeDtypeStruct((rows, heads * HEAD_DIM), jnp.bfloat16)
        out_specs = out_spec
    else:
        out_shape = [jax.ShapeDtypeStruct((rows, heads * HEAD_DIM), jnp.float32)] * 3
        out_specs = [out_spec] * 3
    return pl.pallas_call(
        kernel,
        out_shape=out_shape,
        grid=(heads,),
        in_specs=in_specs,
        out_specs=out_specs,
        compiler_params=pltpu.CompilerParams(dimension_semantics=("arbitrary",)),
    )(*operands)


def per_device(tokens, modulation, w_qkv, w_out, adjacency):
    inputs = tokens[0, 0].astype(jnp.float32)
    width = inputs.shape[1]
    half_heads = w_qkv.shape[2]
    heads = half_heads // HEAD_DIM
    shift_scale = modulation[0]
    squares = jnp.mean(inputs * inputs, axis=1, keepdims=True)
    normed = (inputs * lax.rsqrt(squares + 1e-06) * (1.0 + shift_scale[1]) + shift_scale[0]).astype(
        jnp.bfloat16
    )
    half_rows = normed.shape[0]
    partner_normed = swap(normed, "tp")
    flat_w = w_qkv.reshape(width, 3 * half_heads)
    qkv_own = jnp.dot(normed, flat_w, preferred_element_type=jnp.float32).astype(jnp.bfloat16)
    pair_own = qkv_own[:, half_heads:]
    qkv_other = jnp.dot(partner_normed, flat_w, preferred_element_type=jnp.float32).astype(
        jnp.bfloat16
    )
    pair_other = qkv_other[:, half_heads:]
    queries = jnp.concatenate([qkv_own[:, :half_heads], qkv_other[:, :half_heads]], axis=0)

    received = {}
    for sign in (1, -1):
        near = [from_behind(piece, "orbit", -sign) for piece in (pair_own, pair_other)]
        far = [from_behind(piece, "orbit", -sign) for piece in near]
        received[sign] = near
        received[2 * sign] = far

    tp_index = lax.axis_index("tp")
    flags = adjacency[0]
    blocks = flags.shape[1]
    per_chunk = blocks // 2
    own_start = tp_index * per_chunk
    other_start = (1 - tp_index) * per_chunk

    def chunk_bias(offsets):
        rows_of = []
        for offset in offsets:
            row = flags[offset + REACH if offset < 0 else offset + REACH - 1]
            rows_of.append(lax.dynamic_slice_in_dim(row, own_start, per_chunk))
            rows_of.append(lax.dynamic_slice_in_dim(row, other_start, per_chunk))
        allowed = jnp.repeat(jnp.concatenate(rows_of), BLOCK) > 0
        return jnp.where(allowed, 0.0, -1e30).astype(jnp.float32)[None, :]

    carry = attend_stage(
        queries, [pair_own, pair_other], None, None, first=True, last=False, heads=heads
    )
    carry = attend_stage(
        queries, received[-1] + received[1], chunk_bias((-1, 1)), carry,
        first=False, last=False, heads=heads,
    )
    far_chunks = received[-2] + received[2]
    far_bias = chunk_bias((-2, 2))
    context_other = attend_stage(
        queries, far_chunks, far_bias, carry,
        first=False, last=True, heads=heads, row_block=1, rows=half_rows,
    )
    context_own = attend_stage(
        queries, far_chunks, far_bias, carry,
        first=False, last=True, heads=heads, row_block=0, rows=half_rows,
    )

    owner = lax.axis_index("cfg")
    half_width = width // 2
    weight_now = jnp.where(owner == 0, guide_scale, 1.0 - guide_scale).astype(jnp.float32)
    w_mine = lax.dynamic_slice_in_dim(w_out, owner * half_width, half_width, 1)
    w_theirs = lax.dynamic_slice_in_dim(w_out, (1 - owner) * half_width, half_width, 1)

    def project(context):
        theirs = weight_now * jnp.dot(context, w_theirs, preferred_element_type=jnp.float32)
        mine = weight_now * jnp.dot(context, w_mine, preferred_element_type=jnp.float32)
        return mine + swap(theirs, "cfg")

    guided = project(context_own) + swap(project(context_other), "tp")
    return guided.astype(jnp.bfloat16)[None]


def solution(mesh):
    return jax.shard_map(
        per_device,
        mesh=mesh,
        in_specs=(
            P("cfg", "orbit", "tp", None),
            P("cfg", None, None),
            P(None, None, "tp"),
            P("tp", None),
            P("orbit", None, None),
        ),
        out_specs=P("orbit", "tp", "cfg"),
        check_vma=False,
    )
```

```python
import functools

import jax
import jax.numpy as jnp
from jax import lax
from jax.experimental import pallas as pl
from jax.experimental.pallas import tpu as pltpu
from jax.sharding import PartitionSpec as P

HEAD_DIM = 128
REACH = 2
BLOCK = 128


guide_scale = 4.0


def from_behind(array, axis, by):
    count = lax.axis_size(axis)
    return lax.ppermute(array, axis, [(i, (i + by) % count) for i in range(count)])


def swap(array, axis):
    return lax.ppermute(array, axis, [(0, 1), (1, 0)])


def stage_kernel(*refs, n_chunks, first, last, masked, scale):
    refs = list(refs)
    bias_ref = refs.pop(0) if masked else None
    q_ref = refs.pop(0)
    chunk_refs = refs[: 2 * n_chunks]
    rest = refs[2 * n_chunks :]
    if first:
        outs = rest
    else:
        m_in, l_in, acc_in = rest[:3]
        outs = rest[3:]
    q = q_ref[...]
    rows = q.shape[0]
    if first:
        m = jnp.full((rows, HEAD_DIM), -jnp.inf, jnp.float32)
        l = jnp.zeros((rows, HEAD_DIM), jnp.float32)
        acc = jnp.zeros((rows, HEAD_DIM), jnp.float32)
    else:
        m = m_in[...]
        l = l_in[...]
        acc = acc_in[...]
    for index in range(n_chunks):
        keys = chunk_refs[2 * index][...]
        values = chunk_refs[2 * index + 1][...]
        width = keys.shape[0]
        scores = lax.dot_general(
            q, keys, (((1,), (1,)), ((), ())), preferred_element_type=jnp.float32
        ) * scale
        if masked:
            scores = scores + bias_ref[:, index * width : (index + 1) * width]
        m_new = jnp.maximum(m, jnp.max(scores, axis=1, keepdims=True))
        alpha = jnp.exp(m - m_new)
        expon = jnp.exp(scores - jnp.tile(m_new, (1, width // HEAD_DIM)))
        l = alpha * l + jnp.sum(expon, axis=1, keepdims=True)
        acc = alpha * acc + jnp.dot(
            expon.astype(jnp.bfloat16), values, preferred_element_type=jnp.float32
        )
        m = m_new
    if last:
        outs[0][...] = (acc / l).astype(outs[0].dtype)
    else:
        outs[0][...] = m
        outs[1][...] = l
        outs[2][...] = acc


def attend_stage(queries, chunks, bias, carry, *, first, last, heads, row_block=0, rows=None):
    rows = queries.shape[0] if rows is None else rows
    n_chunks = len(chunks)
    masked = bias is not None
    kernel = functools.partial(
        stage_kernel,
        n_chunks=n_chunks,
        first=first,
        last=last,
        masked=masked,
        scale=HEAD_DIM ** (-0.5),
    )
    row_spec = pl.BlockSpec((rows, HEAD_DIM), lambda h: (row_block, h))
    in_specs = []
    operands = []
    if masked:
        in_specs.append(pl.BlockSpec(bias.shape, lambda h: (0, 0)))
        operands.append(bias)
    in_specs.append(row_spec)
    operands.append(queries)
    for chunk in chunks:
        width = chunk.shape[0]
        in_specs.append(pl.BlockSpec((width, HEAD_DIM), lambda h: (0, h)))
        in_specs.append(pl.BlockSpec((width, HEAD_DIM), lambda h: (0, heads + h)))
        operands += [chunk, chunk]
    if not first:
        in_specs += [row_spec] * 3
        operands += list(carry)
    out_spec = pl.BlockSpec((rows, HEAD_DIM), lambda h: (0, h))
    if last:
        out_shape = jax.ShapeDtypeStruct((rows, heads * HEAD_DIM), jnp.bfloat16)
        out_specs = out_spec
    else:
        out_shape = [jax.ShapeDtypeStruct((rows, heads * HEAD_DIM), jnp.float32)] * 3
        out_specs = [out_spec] * 3
    return pl.pallas_call(
        kernel,
        out_shape=out_shape,
        grid=(heads,),
        in_specs=in_specs,
        out_specs=out_specs,
        compiler_params=pltpu.CompilerParams(dimension_semantics=("arbitrary",)),
    )(*operands)


def per_device(tokens, modulation, w_qkv, w_out, adjacency):
    inputs = tokens[0, 0].astype(jnp.float32)
    width = inputs.shape[1]
    half_heads = w_qkv.shape[2]
    heads = half_heads // HEAD_DIM
    shift_scale = modulation[0]
    squares = jnp.mean(inputs * inputs, axis=1, keepdims=True)
    normed = (inputs * lax.rsqrt(squares + 1e-06) * (1.0 + shift_scale[1]) + shift_scale[0]).astype(
        jnp.bfloat16
    )
    half_rows = normed.shape[0]
    partner_normed = swap(normed, "tp")
    flat_w = w_qkv.reshape(width, 3 * half_heads)
    qkv_own = jnp.dot(normed, flat_w, preferred_element_type=jnp.float32).astype(jnp.bfloat16)
    pair_own = qkv_own[:, half_heads:]
    qkv_other = jnp.dot(partner_normed, flat_w, preferred_element_type=jnp.float32).astype(
        jnp.bfloat16
    )
    pair_other = qkv_other[:, half_heads:]
    queries = jnp.concatenate([qkv_own[:, :half_heads], qkv_other[:, :half_heads]], axis=0)

    received = {}
    for sign in (1, -1):
        near = [from_behind(piece, "orbit", -sign) for piece in (pair_own, pair_other)]
        far = [from_behind(piece, "orbit", -sign) for piece in near]
        received[sign] = near
        received[2 * sign] = far

    tp_index = lax.axis_index("tp")
    flags = adjacency[0]
    blocks = flags.shape[1]
    per_chunk = blocks // 2
    own_start = tp_index * per_chunk
    other_start = (1 - tp_index) * per_chunk

    def chunk_bias(offsets):
        rows_of = []
        for offset in offsets:
            row = flags[offset + REACH if offset < 0 else offset + REACH - 1]
            rows_of.append(lax.dynamic_slice_in_dim(row, own_start, per_chunk))
            rows_of.append(lax.dynamic_slice_in_dim(row, other_start, per_chunk))
        allowed = jnp.repeat(jnp.concatenate(rows_of), BLOCK) > 0
        return jnp.where(allowed, 0.0, -1e30).astype(jnp.float32)[None, :]

    carry = attend_stage(
        queries, [pair_own, pair_other], None, None, first=True, last=False, heads=heads
    )
    carry = attend_stage(
        queries, received[-1] + received[1], chunk_bias((-1, 1)), carry,
        first=False, last=False, heads=heads,
    )
    far_chunks = received[-2] + received[2]
    far_bias = chunk_bias((-2, 2))
    context_other = attend_stage(
        queries, far_chunks, far_bias, carry,
        first=False, last=True, heads=heads, row_block=1, rows=half_rows,
    )
    context_own = attend_stage(
        queries, far_chunks, far_bias, carry,
        first=False, last=True, heads=heads, row_block=0, rows=half_rows,
    )

    owner = lax.axis_index("cfg")
    half_width = width // 2
    weight_now = jnp.where(owner == 0, guide_scale, 1.0 - guide_scale).astype(jnp.float32)
    w_mine = lax.dynamic_slice_in_dim(w_out, owner * half_width, half_width, 1)
    w_theirs = lax.dynamic_slice_in_dim(w_out, (1 - owner) * half_width, half_width, 1)

    def project(context):
        theirs = weight_now * jnp.dot(context, w_theirs, preferred_element_type=jnp.float32)
        mine = weight_now * jnp.dot(context, w_mine, preferred_element_type=jnp.float32)
        return mine + swap(theirs, "cfg")

    guided = project(context_own) + swap(project(context_other), "tp")
    return guided.astype(jnp.bfloat16)[None]


def solution(mesh):
    return jax.shard_map(
        per_device,
        mesh=mesh,
        in_specs=(
            P("cfg", "orbit", "tp", None),
            P("cfg", None, None),
            P(None, None, "tp"),
            P("tp", None),
            P("orbit", None, None),
        ),
        out_specs=P("orbit", "tp", "cfg"),
        check_vma=False,
    )
```

```python
import functools

import jax
import jax.numpy as jnp
from jax import lax
from jax.experimental import pallas as pl
from jax.experimental.pallas import tpu as pltpu
from jax.sharding import PartitionSpec as P

HEAD_DIM = 128
REACH = 2
BLOCK = 128


guide_scale = 4.0


def from_behind(array, axis, by):
    count = lax.axis_size(axis)
    return lax.ppermute(array, axis, [(i, (i + by) % count) for i in range(count)])


def swap(array, axis):
    return lax.ppermute(array, axis, [(0, 1), (1, 0)])


def stage_kernel(*refs, n_chunks, first, last, masked, scale):
    refs = list(refs)
    bias_ref = refs.pop(0) if masked else None
    q_ref = refs.pop(0)
    chunk_refs = refs[: 2 * n_chunks]
    rest = refs[2 * n_chunks :]
    if first:
        outs = rest
    else:
        m_in, l_in, acc_in = rest[:3]
        outs = rest[3:]
    q = q_ref[...]
    rows = q.shape[0]
    if first:
        m = jnp.full((rows, HEAD_DIM), -jnp.inf, jnp.float32)
        l = jnp.zeros((rows, HEAD_DIM), jnp.float32)
        acc = jnp.zeros((rows, HEAD_DIM), jnp.float32)
    else:
        m = m_in[...]
        l = l_in[...]
        acc = acc_in[...]
    for index in range(n_chunks):
        keys = chunk_refs[2 * index][...]
        values = chunk_refs[2 * index + 1][...]
        width = keys.shape[0]
        scores = lax.dot_general(
            q, keys, (((1,), (1,)), ((), ())), preferred_element_type=jnp.float32
        ) * scale
        if masked:
            scores = scores + bias_ref[:, index * width : (index + 1) * width]
        m_new = jnp.maximum(m, jnp.max(scores, axis=1, keepdims=True))
        alpha = jnp.exp(m - m_new)
        expon = jnp.exp(scores - jnp.tile(m_new, (1, width // HEAD_DIM)))
        l = alpha * l + jnp.sum(expon, axis=1, keepdims=True)
        acc = alpha * acc + jnp.dot(
            expon.astype(jnp.bfloat16), values, preferred_element_type=jnp.float32
        )
        m = m_new
    if last:
        outs[0][...] = (acc / l).astype(outs[0].dtype)
    else:
        outs[0][...] = m
        outs[1][...] = l
        outs[2][...] = acc


def attend_stage(queries, chunks, bias, carry, *, first, last, heads, row_block=0, rows=None):
    rows = queries.shape[0] if rows is None else rows
    n_chunks = len(chunks)
    masked = bias is not None
    kernel = functools.partial(
        stage_kernel,
        n_chunks=n_chunks,
        first=first,
        last=last,
        masked=masked,
        scale=HEAD_DIM ** (-0.5),
    )
    row_spec = pl.BlockSpec((rows, HEAD_DIM), lambda h: (row_block, h))
    in_specs = []
    operands = []
    if masked:
        in_specs.append(pl.BlockSpec(bias.shape, lambda h: (0, 0)))
        operands.append(bias)
    in_specs.append(row_spec)
    operands.append(queries)
    for chunk in chunks:
        width = chunk.shape[0]
        in_specs.append(pl.BlockSpec((width, HEAD_DIM), lambda h: (0, h)))
        in_specs.append(pl.BlockSpec((width, HEAD_DIM), lambda h: (0, heads + h)))
        operands += [chunk, chunk]
    if not first:
        in_specs += [row_spec] * 3
        operands += list(carry)
    out_spec = pl.BlockSpec((rows, HEAD_DIM), lambda h: (0, h))
    if last:
        out_shape = jax.ShapeDtypeStruct((rows, heads * HEAD_DIM), jnp.bfloat16)
        out_specs = out_spec
    else:
        out_shape = [jax.ShapeDtypeStruct((rows, heads * HEAD_DIM), jnp.float32)] * 3
        out_specs = [out_spec] * 3
    return pl.pallas_call(
        kernel,
        out_shape=out_shape,
        grid=(heads,),
        in_specs=in_specs,
        out_specs=out_specs,
        compiler_params=pltpu.CompilerParams(dimension_semantics=("arbitrary",)),
    )(*operands)


def per_device(tokens, modulation, w_qkv, w_out, adjacency):
    inputs = tokens[0, 0].astype(jnp.float32)
    width = inputs.shape[1]
    half_heads = w_qkv.shape[2]
    heads = half_heads // HEAD_DIM
    shift_scale = modulation[0]
    squares = jnp.mean(inputs * inputs, axis=1, keepdims=True)
    normed = (inputs * lax.rsqrt(squares + 1e-06) * (1.0 + shift_scale[1]) + shift_scale[0]).astype(
        jnp.bfloat16
    )
    half_rows = normed.shape[0]
    partner_normed = swap(normed, "tp")
    w_partner = swap(w_out, "tp")
    flat_w = w_qkv.reshape(width, 3 * half_heads)
    qkv_own = jnp.dot(normed, flat_w, preferred_element_type=jnp.float32).astype(jnp.bfloat16)
    pair_own = qkv_own[:, half_heads:]

    near_own = {sign: from_behind(pair_own, "orbit", -sign) for sign in (1, -1)}

    qkv_other = jnp.dot(partner_normed, flat_w, preferred_element_type=jnp.float32).astype(
        jnp.bfloat16
    )
    pair_other = qkv_other[:, half_heads:]
    queries = jnp.concatenate([qkv_own[:, :half_heads], qkv_other[:, :half_heads]], axis=0)

    tp_index = lax.axis_index("tp")
    flags = adjacency[0]
    blocks = flags.shape[1]
    per_chunk = blocks // 2
    own_start = tp_index * per_chunk
    other_start = (1 - tp_index) * per_chunk

    def chunk_bias(offsets, start):
        rows_of = []
        for offset in offsets:
            row = flags[offset + REACH if offset < 0 else offset + REACH - 1]
            rows_of.append(lax.dynamic_slice_in_dim(row, start, per_chunk))
        allowed = jnp.repeat(jnp.concatenate(rows_of), BLOCK) > 0
        return jnp.where(allowed, 0.0, -1e30).astype(jnp.float32)[None, :]

    carry = attend_stage(
        queries, [pair_own, pair_other], None, None, first=True, last=False, heads=heads
    )
    pair_other, carry = lax.optimization_barrier((pair_other, carry))
    near_other = {sign: from_behind(pair_other, "orbit", -sign) for sign in (1, -1)}
    far_own = {sign: from_behind(near_own[sign], "orbit", -sign) for sign in (1, -1)}
    carry = attend_stage(
        queries, [near_own[-1], near_own[1]], chunk_bias((-1, 1), own_start), carry,
        first=False, last=False, heads=heads,
    )
    far_other = {sign: from_behind(near_other[sign], "orbit", -sign) for sign in (1, -1)}
    carry = attend_stage(
        queries, [near_other[-1], near_other[1]], chunk_bias((-1, 1), other_start), carry,
        first=False, last=False, heads=heads,
    )
    carry = attend_stage(
        queries, [far_own[-1], far_own[1]], chunk_bias((-2, 2), own_start), carry,
        first=False, last=False, heads=heads,
    )
    last_chunks = [far_other[-1], far_other[1]]
    last_bias = chunk_bias((-2, 2), other_start)
    context_other = attend_stage(
        queries, last_chunks, last_bias, carry,
        first=False, last=True, heads=heads, row_block=1, rows=half_rows,
    )
    context_partner = swap(context_other, "tp")
    context_own = attend_stage(
        queries, last_chunks, last_bias, carry,
        first=False, last=True, heads=heads, row_block=0, rows=half_rows,
    )
    context = jnp.concatenate([context_own, context_partner], axis=1)
    w_local = jnp.concatenate([w_out, w_partner], axis=0)

    owner = lax.axis_index("cfg")
    half_width = width // 2
    weight_now = jnp.where(owner == 0, guide_scale, 1.0 - guide_scale).astype(jnp.float32)
    weight_other = jnp.where(owner == 0, 1.0 - guide_scale, guide_scale).astype(jnp.float32)
    w_mine = lax.dynamic_slice_in_dim(w_local, owner * half_width, half_width, 1)
    w_theirs = lax.dynamic_slice_in_dim(w_local, (1 - owner) * half_width, half_width, 1)
    theirs = jnp.dot(context, w_theirs, preferred_element_type=jnp.float32).astype(jnp.bfloat16)
    mine = jnp.dot(context, w_mine, preferred_element_type=jnp.float32).astype(jnp.bfloat16)
    received = swap(theirs, "cfg")
    guided = weight_now * mine.astype(jnp.float32) + weight_other * received.astype(jnp.float32)
    return guided.astype(jnp.bfloat16)[None]


def solution(mesh):
    return jax.shard_map(
        per_device,
        mesh=mesh,
        in_specs=(
            P("cfg", "orbit", "tp", None),
            P("cfg", None, None),
            P(None, None, "tp"),
            P("tp", None),
            P("orbit", None, None),
        ),
        out_specs=P("orbit", "tp", "cfg"),
        check_vma=False,
    )
```

```python
import functools

import jax
import jax.numpy as jnp
from jax import lax
from jax.experimental import pallas as pl
from jax.experimental.pallas import tpu as pltpu
from jax.sharding import PartitionSpec as P


HEAD_DIM = 128
REACH = 2
BLOCK = 128


guide_scale = 4.0


def from_behind(array, axis, by):
    count = lax.axis_size(axis)
    return lax.ppermute(array, axis, [(i, (i + by) % count) for i in range(count)])


def swap(array, axis):
    return lax.ppermute(array, axis, [(0, 1), (1, 0)])


def stage_kernel(*refs, n_chunks, first, last, masked, scale):
    refs = list(refs)
    bias_ref = refs.pop(0) if masked else None
    q_ref = refs.pop(0)
    chunk_refs = refs[: 2 * n_chunks]
    rest = refs[2 * n_chunks :]
    if first:
        outs = rest
    else:
        m_in, l_in, acc_in = rest[:3]
        outs = rest[3:]
    q = q_ref[...]
    rows = q.shape[0]
    if first:
        m = jnp.full((rows, HEAD_DIM), -jnp.inf, jnp.float32)
        l = jnp.zeros((rows, HEAD_DIM), jnp.float32)
        acc = jnp.zeros((rows, HEAD_DIM), jnp.float32)
    else:
        m = m_in[...]
        l = l_in[...]
        acc = acc_in[...]
    for index in range(n_chunks):
        keys = chunk_refs[2 * index][...]
        values = chunk_refs[2 * index + 1][...]
        width = keys.shape[0]
        scores = lax.dot_general(
            q, keys, (((1,), (1,)), ((), ())), preferred_element_type=jnp.float32
        ) * scale
        if masked:
            scores = scores + bias_ref[:, index * width : (index + 1) * width]
        m_new = jnp.maximum(m, jnp.max(scores, axis=1, keepdims=True))
        alpha = jnp.exp(m - m_new)
        expon = jnp.exp(scores - jnp.tile(m_new, (1, width // HEAD_DIM)))
        l = alpha * l + jnp.sum(expon, axis=1, keepdims=True)
        acc = alpha * acc + jnp.dot(
            expon.astype(jnp.bfloat16), values, preferred_element_type=jnp.float32
        )
        m = m_new
    if last:
        outs[0][...] = (acc / l).astype(outs[0].dtype)
    else:
        outs[0][...] = m
        outs[1][...] = l
        outs[2][...] = acc


def attend_stage(queries, chunks, bias, carry, *, first, last, heads, row_block=0, rows=None):
    rows = queries.shape[0] if rows is None else rows
    n_chunks = len(chunks)
    masked = bias is not None
    kernel = functools.partial(
        stage_kernel,
        n_chunks=n_chunks,
        first=first,
        last=last,
        masked=masked,
        scale=HEAD_DIM ** (-0.5),
    )
    row_spec = pl.BlockSpec((rows, HEAD_DIM), lambda h: (row_block, h))
    in_specs = []
    operands = []
    if masked:
        in_specs.append(pl.BlockSpec(bias.shape, lambda h: (0, 0)))
        operands.append(bias)
    in_specs.append(row_spec)
    operands.append(queries)
    for chunk in chunks:
        width = chunk.shape[0]
        in_specs.append(pl.BlockSpec((width, HEAD_DIM), lambda h: (0, h)))
        in_specs.append(pl.BlockSpec((width, HEAD_DIM), lambda h: (0, heads + h)))
        operands += [chunk, chunk]
    if not first:
        in_specs += [row_spec] * 3
        operands += list(carry)
    out_spec = pl.BlockSpec((rows, HEAD_DIM), lambda h: (0, h))
    if last:
        out_shape = jax.ShapeDtypeStruct((rows, heads * HEAD_DIM), jnp.bfloat16)
        out_specs = out_spec
    else:
        out_shape = [jax.ShapeDtypeStruct((rows, heads * HEAD_DIM), jnp.float32)] * 3
        out_specs = [out_spec] * 3
    return pl.pallas_call(
        kernel,
        out_shape=out_shape,
        grid=(heads,),
        in_specs=in_specs,
        out_specs=out_specs,
        compiler_params=pltpu.CompilerParams(dimension_semantics=("arbitrary",)),
    )(*operands)


def per_device_body(tokens, modulation, w_qkv, w_out, adjacency):
    inputs = tokens[0, 0].astype(jnp.float32)
    width = inputs.shape[1]
    half_heads = w_qkv.shape[2]
    heads = half_heads // HEAD_DIM
    shift_scale = modulation[0]
    squares = jnp.mean(inputs * inputs, axis=1, keepdims=True)
    normed = (inputs * lax.rsqrt(squares + 1e-06) * (1.0 + shift_scale[1]) + shift_scale[0]).astype(
        jnp.bfloat16
    )
    half_rows = normed.shape[0]
    partner_normed = swap(normed, "tp")
    flat_w = w_qkv.reshape(width, 3 * half_heads)
    qkv_own = jnp.dot(normed, flat_w, preferred_element_type=jnp.float32).astype(jnp.bfloat16)
    pair_own = qkv_own[:, half_heads:]

    near_own = {sign: from_behind(pair_own, "orbit", -sign) for sign in (1, -1)}

    qkv_other = jnp.dot(partner_normed, flat_w, preferred_element_type=jnp.float32).astype(
        jnp.bfloat16
    )
    pair_other = qkv_other[:, half_heads:]
    queries = jnp.concatenate([qkv_own[:, :half_heads], qkv_other[:, :half_heads]], axis=0)

    tp_index = lax.axis_index("tp")
    flags = adjacency[0]
    blocks = flags.shape[1]
    per_chunk = blocks // 2
    own_start = tp_index * per_chunk
    other_start = (1 - tp_index) * per_chunk

    def chunk_bias(offsets, start):
        rows_of = []
        for offset in offsets:
            row = flags[offset + REACH if offset < 0 else offset + REACH - 1]
            rows_of.append(lax.dynamic_slice_in_dim(row, start, per_chunk))
        allowed = jnp.repeat(jnp.concatenate(rows_of), BLOCK) > 0
        return jnp.where(allowed, 0.0, -1e30).astype(jnp.float32)[None, :]

    carry = attend_stage(
        queries, [pair_own, pair_other], None, None, first=True, last=False, heads=heads
    )
    pair_other, carry = lax.optimization_barrier((pair_other, carry))
    near_other = {sign: from_behind(pair_other, "orbit", -sign) for sign in (1, -1)}
    far_own = {sign: from_behind(near_own[sign], "orbit", -sign) for sign in (1, -1)}
    carry = attend_stage(
        queries, [near_own[-1], near_own[1]], chunk_bias((-1, 1), own_start), carry,
        first=False, last=False, heads=heads,
    )
    far_other = {sign: from_behind(near_other[sign], "orbit", -sign) for sign in (1, -1)}
    carry = attend_stage(
        queries, [near_other[-1], near_other[1]], chunk_bias((-1, 1), other_start), carry,
        first=False, last=False, heads=heads,
    )
    carry = attend_stage(
        queries, [far_own[-1], far_own[1]], chunk_bias((-2, 2), own_start), carry,
        first=False, last=False, heads=heads,
    )
    last_chunks = [far_other[-1], far_other[1]]
    last_bias = chunk_bias((-2, 2), other_start)
    context_other = attend_stage(
        queries, last_chunks, last_bias, carry,
        first=False, last=True, heads=heads, row_block=1, rows=half_rows,
    )
    owner = lax.axis_index("cfg")
    half_width = width // 2
    weight_now = jnp.where(owner == 0, guide_scale, 1.0 - guide_scale).astype(jnp.float32)
    w_mine = lax.dynamic_slice_in_dim(w_out, owner * half_width, half_width, 1)
    w_theirs = lax.dynamic_slice_in_dim(w_out, (1 - owner) * half_width, half_width, 1)

    def project(context):
        theirs = weight_now * jnp.dot(context, w_theirs, preferred_element_type=jnp.float32)
        mine = weight_now * jnp.dot(context, w_mine, preferred_element_type=jnp.float32)
        return mine + swap(theirs, "cfg")

    to_partner = project(context_other).astype(jnp.bfloat16)
    to_partner, carry = lax.optimization_barrier((to_partner, carry))
    from_partner = swap(to_partner, "tp")
    context_own = attend_stage(
        queries, last_chunks, last_bias, carry,
        first=False, last=True, heads=heads, row_block=0, rows=half_rows,
    )
    guided = project(context_own) + from_partner.astype(jnp.float32)
    return guided.astype(jnp.bfloat16)[None]


def solution(mesh):
    return jax.shard_map(
        per_device_body,
        mesh=mesh,
        in_specs=(
            P("cfg", "orbit", "tp", None),
            P("cfg", None, None),
            P(None, None, "tp"),
            P("tp", None),
            P("orbit", None, None),
        ),
        out_specs=P("orbit", "tp", "cfg"),
        check_vma=False,
    )
```

```python
import functools

import jax
import jax.numpy as jnp
from jax import lax
from jax.experimental import pallas as pl
from jax.experimental.pallas import tpu as pltpu
from jax.sharding import PartitionSpec as P


HEAD_DIM = 128
REACH = 2
BLOCK = 128


guide_scale = 4.0


def from_behind(array, axis, by):
    count = lax.axis_size(axis)
    return lax.ppermute(array, axis, [(i, (i + by) % count) for i in range(count)])


def swap(array, axis):
    return lax.ppermute(array, axis, [(0, 1), (1, 0)])


def stage_kernel(*refs, n_chunks, first, last, masked, scale):
    refs = list(refs)
    bias_ref = refs.pop(0) if masked else None
    q_ref = refs.pop(0)
    chunk_refs = refs[: 2 * n_chunks]
    rest = refs[2 * n_chunks :]
    if first:
        outs = rest
    else:
        m_in, l_in, acc_in = rest[:3]
        outs = rest[3:]
    q = q_ref[...]
    rows = q.shape[0]
    if first:
        m = jnp.full((rows, HEAD_DIM), -jnp.inf, jnp.float32)
        l = jnp.zeros((rows, HEAD_DIM), jnp.float32)
        acc = jnp.zeros((rows, HEAD_DIM), jnp.float32)
    else:
        m = m_in[...]
        l = l_in[...]
        acc = acc_in[...]
    for index in range(n_chunks):
        keys = chunk_refs[2 * index][...]
        values = chunk_refs[2 * index + 1][...]
        width = keys.shape[0]
        scores = lax.dot_general(
            q, keys, (((1,), (1,)), ((), ())), preferred_element_type=jnp.float32
        ) * scale
        if masked:
            scores = scores + bias_ref[:, index * width : (index + 1) * width]
        m_new = jnp.maximum(m, jnp.max(scores, axis=1, keepdims=True))
        alpha = jnp.exp(m - m_new)
        expon = jnp.exp(scores - jnp.tile(m_new, (1, width // HEAD_DIM)))
        l = alpha * l + jnp.sum(expon, axis=1, keepdims=True)
        acc = alpha * acc + jnp.dot(
            expon.astype(jnp.bfloat16), values, preferred_element_type=jnp.float32
        )
        m = m_new
    if last:
        outs[0][...] = (acc / l).astype(outs[0].dtype)
    else:
        outs[0][...] = m
        outs[1][...] = l
        outs[2][...] = acc


def attend_stage(queries, chunks, bias, carry, *, first, last, heads, row_block=0, rows=None):
    rows = queries.shape[0] if rows is None else rows
    n_chunks = len(chunks)
    masked = bias is not None
    kernel = functools.partial(
        stage_kernel,
        n_chunks=n_chunks,
        first=first,
        last=last,
        masked=masked,
        scale=HEAD_DIM ** (-0.5),
    )
    row_spec = pl.BlockSpec((rows, HEAD_DIM), lambda h: (row_block, h))
    in_specs = []
    operands = []
    if masked:
        in_specs.append(pl.BlockSpec(bias.shape, lambda h: (0, 0)))
        operands.append(bias)
    in_specs.append(row_spec)
    operands.append(queries)
    for chunk in chunks:
        width = chunk.shape[0]
        in_specs.append(pl.BlockSpec((width, HEAD_DIM), lambda h: (0, h)))
        in_specs.append(pl.BlockSpec((width, HEAD_DIM), lambda h: (0, heads + h)))
        operands += [chunk, chunk]
    if not first:
        in_specs += [row_spec] * 3
        operands += list(carry)
    out_spec = pl.BlockSpec((rows, HEAD_DIM), lambda h: (0, h))
    if last:
        out_shape = jax.ShapeDtypeStruct((rows, heads * HEAD_DIM), jnp.bfloat16)
        out_specs = out_spec
    else:
        out_shape = [jax.ShapeDtypeStruct((rows, heads * HEAD_DIM), jnp.float32)] * 3
        out_specs = [out_spec] * 3
    return pl.pallas_call(
        kernel,
        out_shape=out_shape,
        grid=(heads,),
        in_specs=in_specs,
        out_specs=out_specs,
        compiler_params=pltpu.CompilerParams(dimension_semantics=("arbitrary",)),
    )(*operands)


def per_device_body(tokens, modulation, w_qkv, w_out, adjacency):
    inputs = tokens[0, 0].astype(jnp.float32)
    width = inputs.shape[1]
    half_heads = w_qkv.shape[2]
    heads = half_heads // HEAD_DIM
    shift_scale = modulation[0]
    squares = jnp.mean(inputs * inputs, axis=1, keepdims=True)
    normed = (inputs * lax.rsqrt(squares + 1e-06) * (1.0 + shift_scale[1]) + shift_scale[0]).astype(
        jnp.bfloat16
    )
    half_rows = normed.shape[0]
    partner_normed = swap(normed, "tp")
    near_own = {sign: from_behind(normed, "orbit", -sign) for sign in (1, -1)}
    flat_w = w_qkv.reshape(width, 3 * half_heads)
    kv_w = w_qkv[:, 1:, :].reshape(width, 2 * half_heads)
    near_other = {sign: from_behind(partner_normed, "orbit", -sign) for sign in (1, -1)}
    qkv_own = jnp.dot(normed, flat_w, preferred_element_type=jnp.float32).astype(jnp.bfloat16)
    pair_own = qkv_own[:, half_heads:]
    qkv_other = jnp.dot(partner_normed, flat_w, preferred_element_type=jnp.float32).astype(
        jnp.bfloat16
    )
    pair_other = qkv_other[:, half_heads:]

    def project_pair(rows):
        return jnp.dot(rows, kv_w, preferred_element_type=jnp.float32).astype(jnp.bfloat16)

    near_own = {sign: project_pair(near_own[sign]) for sign in (1, -1)}
    far_own = {sign: from_behind(near_own[sign], "orbit", -sign) for sign in (1, -1)}
    near_other = {sign: project_pair(near_other[sign]) for sign in (1, -1)}
    far_other = {sign: from_behind(near_other[sign], "orbit", -sign) for sign in (1, -1)}
    queries = jnp.concatenate([qkv_own[:, :half_heads], qkv_other[:, :half_heads]], axis=0)

    tp_index = lax.axis_index("tp")
    flags = adjacency[0]
    blocks = flags.shape[1]
    per_chunk = blocks // 2
    own_start = tp_index * per_chunk
    other_start = (1 - tp_index) * per_chunk

    def chunk_bias(offsets, start):
        rows_of = []
        for offset in offsets:
            row = flags[offset + REACH if offset < 0 else offset + REACH - 1]
            rows_of.append(lax.dynamic_slice_in_dim(row, start, per_chunk))
        allowed = jnp.repeat(jnp.concatenate(rows_of), BLOCK) > 0
        return jnp.where(allowed, 0.0, -1e30).astype(jnp.float32)[None, :]

    carry = attend_stage(
        queries, [pair_own, pair_other], None, None, first=True, last=False, heads=heads
    )
    carry = attend_stage(
        queries, [near_own[-1], near_own[1]], chunk_bias((-1, 1), own_start), carry,
        first=False, last=False, heads=heads,
    )
    carry = attend_stage(
        queries, [near_other[-1], near_other[1]], chunk_bias((-1, 1), other_start), carry,
        first=False, last=False, heads=heads,
    )
    carry = attend_stage(
        queries, [far_own[-1], far_own[1]], chunk_bias((-2, 2), own_start), carry,
        first=False, last=False, heads=heads,
    )
    last_chunks = [far_other[-1], far_other[1]]
    last_bias = chunk_bias((-2, 2), other_start)
    context_other = attend_stage(
        queries, last_chunks, last_bias, carry,
        first=False, last=True, heads=heads, row_block=1, rows=half_rows,
    )
    owner = lax.axis_index("cfg")
    half_width = width // 2
    weight_now = jnp.where(owner == 0, guide_scale, 1.0 - guide_scale).astype(jnp.float32)
    w_mine = lax.dynamic_slice_in_dim(w_out, owner * half_width, half_width, 1)
    w_theirs = lax.dynamic_slice_in_dim(w_out, (1 - owner) * half_width, half_width, 1)

    def project(context):
        theirs = weight_now * jnp.dot(context, w_theirs, preferred_element_type=jnp.float32)
        mine = weight_now * jnp.dot(context, w_mine, preferred_element_type=jnp.float32)
        return mine + swap(theirs, "cfg")

    to_partner = project(context_other).astype(jnp.bfloat16)
    to_partner, carry = lax.optimization_barrier((to_partner, carry))
    from_partner = swap(to_partner, "tp")
    context_own = attend_stage(
        queries, last_chunks, last_bias, carry,
        first=False, last=True, heads=heads, row_block=0, rows=half_rows,
    )
    guided = project(context_own) + from_partner.astype(jnp.float32)
    return guided.astype(jnp.bfloat16)[None]


def solution(mesh):
    return jax.shard_map(
        per_device_body,
        mesh=mesh,
        in_specs=(
            P("cfg", "orbit", "tp", None),
            P("cfg", None, None),
            P(None, None, "tp"),
            P("tp", None),
            P("orbit", None, None),
        ),
        out_specs=P("orbit", "tp", "cfg"),
        check_vma=False,
    )
```

```python
import functools

import jax
import jax.numpy as jnp
from jax import lax
from jax.experimental import pallas as pl
from jax.experimental.pallas import tpu as pltpu
from jax.sharding import PartitionSpec as P


HEAD_DIM = 128
REACH = 2
BLOCK = 128


guide_scale = 4.0


def from_behind(array, axis, by):
    count = lax.axis_size(axis)
    return lax.ppermute(array, axis, [(i, (i + by) % count) for i in range(count)])


def swap(array, axis):
    return lax.ppermute(array, axis, [(0, 1), (1, 0)])


def stage_kernel(*refs, n_chunks, first, last, masked, scale):
    refs = list(refs)
    bias_ref = refs.pop(0) if masked else None
    q_ref = refs.pop(0)
    chunk_refs = refs[: 2 * n_chunks]
    rest = refs[2 * n_chunks :]
    if first:
        outs = rest
    else:
        m_in, l_in, acc_in = rest[:3]
        outs = rest[3:]
    q = q_ref[...]
    rows = q.shape[0]
    if first:
        m = jnp.full((rows, HEAD_DIM), -jnp.inf, jnp.float32)
        l = jnp.zeros((rows, HEAD_DIM), jnp.float32)
        acc = jnp.zeros((rows, HEAD_DIM), jnp.float32)
    else:
        m = m_in[...]
        l = l_in[...]
        acc = acc_in[...]
    for index in range(n_chunks):
        keys = chunk_refs[2 * index][...]
        values = chunk_refs[2 * index + 1][...]
        width = keys.shape[0]
        scores = lax.dot_general(
            q, keys, (((1,), (1,)), ((), ())), preferred_element_type=jnp.float32
        ) * scale
        if masked:
            scores = scores + bias_ref[:, index * width : (index + 1) * width]
        m_new = jnp.maximum(m, jnp.max(scores, axis=1, keepdims=True))
        alpha = jnp.exp(m - m_new)
        expon = jnp.exp(scores - jnp.tile(m_new, (1, width // HEAD_DIM)))
        l = alpha * l + jnp.sum(expon, axis=1, keepdims=True)
        acc = alpha * acc + jnp.dot(
            expon.astype(jnp.bfloat16), values, preferred_element_type=jnp.float32
        )
        m = m_new
    if last:
        outs[0][...] = (acc / l).astype(outs[0].dtype)
    else:
        outs[0][...] = m
        outs[1][...] = l
        outs[2][...] = acc


def attend_stage(queries, chunks, bias, carry, *, first, last, heads, row_block=0, rows=None):
    rows = queries.shape[0] if rows is None else rows
    n_chunks = len(chunks)
    masked = bias is not None
    kernel = functools.partial(
        stage_kernel,
        n_chunks=n_chunks,
        first=first,
        last=last,
        masked=masked,
        scale=HEAD_DIM ** (-0.5),
    )
    row_spec = pl.BlockSpec((rows, HEAD_DIM), lambda h: (row_block, h))
    in_specs = []
    operands = []
    if masked:
        in_specs.append(pl.BlockSpec(bias.shape, lambda h: (0, 0)))
        operands.append(bias)
    in_specs.append(row_spec)
    operands.append(queries)
    for chunk in chunks:
        width = chunk.shape[0]
        in_specs.append(pl.BlockSpec((width, HEAD_DIM), lambda h: (0, h)))
        in_specs.append(pl.BlockSpec((width, HEAD_DIM), lambda h: (0, heads + h)))
        operands += [chunk, chunk]
    if not first:
        in_specs += [row_spec] * 3
        operands += list(carry)
    out_spec = pl.BlockSpec((rows, HEAD_DIM), lambda h: (0, h))
    if last:
        out_shape = jax.ShapeDtypeStruct((rows, heads * HEAD_DIM), jnp.bfloat16)
        out_specs = out_spec
    else:
        out_shape = [jax.ShapeDtypeStruct((rows, heads * HEAD_DIM), jnp.float32)] * 3
        out_specs = [out_spec] * 3
    return pl.pallas_call(
        kernel,
        out_shape=out_shape,
        grid=(heads,),
        in_specs=in_specs,
        out_specs=out_specs,
        compiler_params=pltpu.CompilerParams(dimension_semantics=("arbitrary",)),
    )(*operands)


def per_device_body(tokens, modulation, w_qkv, w_out, adjacency):
    inputs = tokens[0, 0].astype(jnp.float32)
    width = inputs.shape[1]
    half_heads = w_qkv.shape[2]
    heads = half_heads // HEAD_DIM
    shift_scale = modulation[0]
    squares = jnp.mean(inputs * inputs, axis=1, keepdims=True)
    normed = (inputs * lax.rsqrt(squares + 1e-06) * (1.0 + shift_scale[1]) + shift_scale[0]).astype(
        jnp.bfloat16
    )
    half_rows = normed.shape[0]
    partner_normed = swap(normed, "tp")
    kv_w = w_qkv[:, 1:, :].reshape(width, 2 * half_heads)
    q_w = w_qkv[:, 0, :]
    pair_own = jnp.dot(normed, kv_w, preferred_element_type=jnp.float32).astype(jnp.bfloat16)

    piece_rows = half_rows // 2
    own_pieces = [pair_own[:piece_rows], pair_own[piece_rows:]]
    near = {sign: [from_behind(piece, "orbit", -sign) for piece in own_pieces] for sign in (1, -1)}

    pair_other = jnp.dot(partner_normed, kv_w, preferred_element_type=jnp.float32).astype(
        jnp.bfloat16
    )
    both_rows = jnp.concatenate([normed, partner_normed], axis=0)
    queries = jnp.dot(both_rows, q_w, preferred_element_type=jnp.float32).astype(jnp.bfloat16)

    tp_index = lax.axis_index("tp")
    flags = adjacency[0]
    blocks = flags.shape[1]
    per_piece = blocks // 4
    own_start = tp_index * 2 * per_piece
    other_start = (1 - tp_index) * 2 * per_piece
    starts = [own_start, own_start + per_piece, other_start, other_start + per_piece]

    def chunk_bias(offsets, piece):
        rows_of = []
        for offset in offsets:
            row = flags[offset + REACH if offset < 0 else offset + REACH - 1]
            rows_of.append(lax.dynamic_slice_in_dim(row, starts[piece], per_piece))
        allowed = jnp.repeat(jnp.concatenate(rows_of), BLOCK) > 0
        return jnp.where(allowed, 0.0, -1e30).astype(jnp.float32)[None, :]

    carry = attend_stage(
        queries, [pair_own, pair_other], None, None, first=True, last=False, heads=heads
    )
    pair_other, carry = lax.optimization_barrier((pair_other, carry))
    for sign in (1, -1):
        near[sign] += [from_behind(pair_other[:piece_rows], "orbit", -sign),
                       from_behind(pair_other[piece_rows:], "orbit", -sign)]
    far = {sign: [from_behind(piece, "orbit", -sign) for piece in near[sign]] for sign in (1, -1)}

    def near_stage(pieces_of, carry):
        chunks = []
        biases = []
        for piece in pieces_of:
            chunks += [near[-1][piece], near[1][piece]]
            biases.append(chunk_bias((-1, 1), piece))
        return attend_stage(
            queries, chunks, jnp.concatenate(biases, axis=1), carry,
            first=False, last=False, heads=heads,
        )

    def far_chunks(pieces_of):
        chunks = []
        biases = []
        for piece in pieces_of:
            chunks += [far[-1][piece], far[1][piece]]
            biases.append(chunk_bias((-2, 2), piece))
        return chunks, jnp.concatenate(biases, axis=1)

    carry = near_stage([0, 1], carry)
    carry = near_stage([2, 3], carry)
    chunks, bias = far_chunks([0, 1])
    carry = attend_stage(queries, chunks, bias, carry, first=False, last=False, heads=heads)
    chunks, bias = far_chunks([2])
    carry = attend_stage(queries, chunks, bias, carry, first=False, last=False, heads=heads)
    last_chunks, last_bias = far_chunks([3])
    context_other = attend_stage(
        queries, last_chunks, last_bias, carry,
        first=False, last=True, heads=heads, row_block=1, rows=half_rows,
    )

    owner = lax.axis_index("cfg")
    half_width = width // 2
    weight_now = jnp.where(owner == 0, guide_scale, 1.0 - guide_scale).astype(jnp.float32)
    w_mine = lax.dynamic_slice_in_dim(w_out, owner * half_width, half_width, 1)
    w_theirs = lax.dynamic_slice_in_dim(w_out, (1 - owner) * half_width, half_width, 1)

    def project(context):
        theirs = weight_now * jnp.dot(context, w_theirs, preferred_element_type=jnp.float32)
        mine = weight_now * jnp.dot(context, w_mine, preferred_element_type=jnp.float32)
        return mine + swap(theirs, "cfg")

    to_partner = project(context_other).astype(jnp.bfloat16)
    to_partner, carry = lax.optimization_barrier((to_partner, carry))
    from_partner = swap(to_partner, "tp")
    context_own = attend_stage(
        queries, last_chunks, last_bias, carry,
        first=False, last=True, heads=heads, row_block=0, rows=half_rows,
    )
    guided = project(context_own) + from_partner.astype(jnp.float32)
    return guided.astype(jnp.bfloat16)[None]


def solution(mesh):
    return jax.shard_map(
        per_device_body,
        mesh=mesh,
        in_specs=(
            P("cfg", "orbit", "tp", None),
            P("cfg", None, None),
            P(None, None, "tp"),
            P("tp", None),
            P("orbit", None, None),
        ),
        out_specs=P("orbit", "tp", "cfg"),
        check_vma=False,
    )
```

```python
import functools

import jax
import jax.numpy as jnp
from jax import lax
from jax.experimental import pallas as pl
from jax.experimental.pallas import tpu as pltpu
from jax.sharding import PartitionSpec as P


HEAD_DIM = 128
REACH = 2
BLOCK = 128


guide_scale = 4.0


def from_behind(array, axis, by):
    count = lax.axis_size(axis)
    return lax.ppermute(array, axis, [(i, (i + by) % count) for i in range(count)])


def swap(array, axis):
    return lax.ppermute(array, axis, [(0, 1), (1, 0)])


def stage_kernel(*refs, n_chunks, first, last, masked, scale):
    refs = list(refs)
    bias_ref = refs.pop(0) if masked else None
    q_ref = refs.pop(0)
    chunk_refs = refs[: 2 * n_chunks]
    rest = refs[2 * n_chunks :]
    if first:
        outs = rest
    else:
        m_in, l_in, acc_in = rest[:3]
        outs = rest[3:]
    q = q_ref[...]
    rows = q.shape[0]
    if first:
        m = jnp.full((rows, HEAD_DIM), -jnp.inf, jnp.float32)
        l = jnp.zeros((rows, HEAD_DIM), jnp.float32)
        acc = jnp.zeros((rows, HEAD_DIM), jnp.float32)
    else:
        m = m_in[...]
        l = l_in[...]
        acc = acc_in[...]
    for index in range(n_chunks):
        keys = chunk_refs[2 * index][...]
        values = chunk_refs[2 * index + 1][...]
        width = keys.shape[0]
        scores = lax.dot_general(
            q, keys, (((1,), (1,)), ((), ())), preferred_element_type=jnp.float32
        ) * scale
        if masked:
            scores = scores + bias_ref[:, index * width : (index + 1) * width]
        m_new = jnp.maximum(m, jnp.max(scores, axis=1, keepdims=True))
        alpha = jnp.exp(m - m_new)
        expon = jnp.exp(scores - jnp.tile(m_new, (1, width // HEAD_DIM)))
        l = alpha * l + jnp.sum(expon, axis=1, keepdims=True)
        acc = alpha * acc + jnp.dot(
            expon.astype(jnp.bfloat16), values, preferred_element_type=jnp.float32
        )
        m = m_new
    if last:
        outs[0][...] = (acc / l).astype(outs[0].dtype)
    else:
        outs[0][...] = m
        outs[1][...] = l
        outs[2][...] = acc


def attend_stage(queries, chunks, bias, carry, *, first, last, heads, row_block=0, rows=None):
    rows = queries.shape[0] if rows is None else rows
    n_chunks = len(chunks)
    masked = bias is not None
    kernel = functools.partial(
        stage_kernel,
        n_chunks=n_chunks,
        first=first,
        last=last,
        masked=masked,
        scale=HEAD_DIM ** (-0.5),
    )
    row_spec = pl.BlockSpec((rows, HEAD_DIM), lambda h: (row_block, h))
    in_specs = []
    operands = []
    if masked:
        in_specs.append(pl.BlockSpec(bias.shape, lambda h: (0, 0)))
        operands.append(bias)
    in_specs.append(row_spec)
    operands.append(queries)
    for chunk in chunks:
        width = chunk.shape[0]
        in_specs.append(pl.BlockSpec((width, HEAD_DIM), lambda h: (0, h)))
        in_specs.append(pl.BlockSpec((width, HEAD_DIM), lambda h: (0, heads + h)))
        operands += [chunk, chunk]
    if not first:
        in_specs += [row_spec] * 3
        operands += list(carry)
    out_spec = pl.BlockSpec((rows, HEAD_DIM), lambda h: (0, h))
    if last:
        out_shape = jax.ShapeDtypeStruct((rows, heads * HEAD_DIM), jnp.bfloat16)
        out_specs = out_spec
    else:
        out_shape = [jax.ShapeDtypeStruct((rows, heads * HEAD_DIM), jnp.float32)] * 3
        out_specs = [out_spec] * 3
    return pl.pallas_call(
        kernel,
        out_shape=out_shape,
        grid=(heads,),
        in_specs=in_specs,
        out_specs=out_specs,
        compiler_params=pltpu.CompilerParams(dimension_semantics=("arbitrary",)),
    )(*operands)


def per_device_body(tokens, modulation, w_qkv, w_out, adjacency):
    inputs = tokens[0, 0].astype(jnp.float32)
    width = inputs.shape[1]
    half_heads = w_qkv.shape[2]
    heads = half_heads // HEAD_DIM
    shift_scale = modulation[0]
    squares = jnp.mean(inputs * inputs, axis=1, keepdims=True)
    normed = (inputs * lax.rsqrt(squares + 1e-06) * (1.0 + shift_scale[1]) + shift_scale[0]).astype(
        jnp.bfloat16
    )
    half_rows = normed.shape[0]
    partner_normed = swap(normed, "tp")
    kv_w = w_qkv[:, 1:, :].reshape(width, 2 * half_heads)
    q_w = w_qkv[:, 0, :]
    pair_own = jnp.dot(normed, kv_w, preferred_element_type=jnp.float32).astype(jnp.bfloat16)

    pair_own, partner_normed = lax.optimization_barrier((pair_own, partner_normed))
    near_own = {sign: from_behind(pair_own, "orbit", -sign) for sign in (1, -1)}

    pair_other = jnp.dot(partner_normed, kv_w, preferred_element_type=jnp.float32).astype(
        jnp.bfloat16
    )
    both_rows = jnp.concatenate([normed, partner_normed], axis=0)
    queries = jnp.dot(both_rows, q_w, preferred_element_type=jnp.float32).astype(jnp.bfloat16)

    tp_index = lax.axis_index("tp")
    flags = adjacency[0]
    blocks = flags.shape[1]
    per_chunk = blocks // 2
    own_start = tp_index * per_chunk
    other_start = (1 - tp_index) * per_chunk

    def chunk_bias(offsets, start):
        rows_of = []
        for offset in offsets:
            row = flags[offset + REACH if offset < 0 else offset + REACH - 1]
            rows_of.append(lax.dynamic_slice_in_dim(row, start, per_chunk))
        allowed = jnp.repeat(jnp.concatenate(rows_of), BLOCK) > 0
        return jnp.where(allowed, 0.0, -1e30).astype(jnp.float32)[None, :]

    carry = attend_stage(
        queries, [pair_own, pair_other], None, None, first=True, last=False, heads=heads
    )
    pair_other, carry = lax.optimization_barrier((pair_other, carry))
    near_other = {sign: from_behind(pair_other, "orbit", -sign) for sign in (1, -1)}
    far_own = {sign: from_behind(near_own[sign], "orbit", -sign) for sign in (1, -1)}
    carry = attend_stage(
        queries, [near_own[-1], near_own[1]], chunk_bias((-1, 1), own_start), carry,
        first=False, last=False, heads=heads,
    )
    far_other = {sign: from_behind(near_other[sign], "orbit", -sign) for sign in (1, -1)}
    carry = attend_stage(
        queries, [near_other[-1], near_other[1]], chunk_bias((-1, 1), other_start), carry,
        first=False, last=False, heads=heads,
    )
    carry = attend_stage(
        queries, [far_own[-1], far_own[1]], chunk_bias((-2, 2), own_start), carry,
        first=False, last=False, heads=heads,
    )
    last_chunks = [far_other[-1], far_other[1]]
    last_bias = chunk_bias((-2, 2), other_start)
    context_other = attend_stage(
        queries, last_chunks, last_bias, carry,
        first=False, last=True, heads=heads, row_block=1, rows=half_rows,
    )
    owner = lax.axis_index("cfg")
    half_width = width // 2
    weight_now = jnp.where(owner == 0, guide_scale, 1.0 - guide_scale).astype(jnp.float32)
    w_mine = lax.dynamic_slice_in_dim(w_out, owner * half_width, half_width, 1)
    w_theirs = lax.dynamic_slice_in_dim(w_out, (1 - owner) * half_width, half_width, 1)

    def project(context):
        theirs = weight_now * jnp.dot(context, w_theirs, preferred_element_type=jnp.float32)
        mine = weight_now * jnp.dot(context, w_mine, preferred_element_type=jnp.float32)
        return mine + swap(theirs, "cfg")

    to_partner = project(context_other).astype(jnp.bfloat16)
    to_partner, carry = lax.optimization_barrier((to_partner, carry))
    from_partner = swap(to_partner, "tp")
    context_own = attend_stage(
        queries, last_chunks, last_bias, carry,
        first=False, last=True, heads=heads, row_block=0, rows=half_rows,
    )
    guided = project(context_own) + from_partner.astype(jnp.float32)
    return guided.astype(jnp.bfloat16)[None]


def solution(mesh):
    return jax.shard_map(
        per_device_body,
        mesh=mesh,
        in_specs=(
            P("cfg", "orbit", "tp", None),
            P("cfg", None, None),
            P(None, None, "tp"),
            P("tp", None),
            P("orbit", None, None),
        ),
        out_specs=P("orbit", "tp", "cfg"),
        check_vma=False,
    )
```

```python
import functools

import jax
import jax.numpy as jnp
from jax import lax
from jax.experimental import pallas as pl
from jax.experimental.pallas import tpu as pltpu
from jax.sharding import PartitionSpec as P


HEAD_DIM = 128
REACH = 2
BLOCK = 128


guide_scale = 4.0


def from_behind(array, axis, by):
    count = lax.axis_size(axis)
    return lax.ppermute(array, axis, [(i, (i + by) % count) for i in range(count)])


def swap(array, axis):
    return lax.ppermute(array, axis, [(0, 1), (1, 0)])


def stage_kernel(*refs, n_chunks, first, last, masked, scale):
    refs = list(refs)
    bias_ref = refs.pop(0) if masked else None
    q_ref = refs.pop(0)
    chunk_refs = refs[: 2 * n_chunks]
    rest = refs[2 * n_chunks :]
    if first:
        outs = rest
    else:
        m_in, l_in, acc_in = rest[:3]
        outs = rest[3:]
    q = q_ref[...]
    rows = q.shape[0]
    if first:
        m = jnp.full((rows, HEAD_DIM), -jnp.inf, jnp.float32)
        l = jnp.zeros((rows, HEAD_DIM), jnp.float32)
        acc = jnp.zeros((rows, HEAD_DIM), jnp.float32)
    else:
        m = m_in[...]
        l = l_in[...]
        acc = acc_in[...]
    for index in range(n_chunks):
        keys = chunk_refs[2 * index][...]
        values = chunk_refs[2 * index + 1][...]
        width = keys.shape[0]
        scores = lax.dot_general(
            q, keys, (((1,), (1,)), ((), ())), preferred_element_type=jnp.float32
        ) * scale
        if masked:
            scores = scores + bias_ref[:, index * width : (index + 1) * width]
        m_new = jnp.maximum(m, jnp.max(scores, axis=1, keepdims=True))
        alpha = jnp.exp(m - m_new)
        expon = jnp.exp(scores - jnp.tile(m_new, (1, width // HEAD_DIM)))
        l = alpha * l + jnp.sum(expon, axis=1, keepdims=True)
        acc = alpha * acc + jnp.dot(
            expon.astype(jnp.bfloat16), values, preferred_element_type=jnp.float32
        )
        m = m_new
    if last:
        outs[0][...] = (acc / l).astype(outs[0].dtype)
    else:
        outs[0][...] = m
        outs[1][...] = l
        outs[2][...] = acc


def attend_stage(queries, chunks, bias, carry, *, first, last, heads, row_block=0, rows=None):
    rows = queries.shape[0] if rows is None else rows
    n_chunks = len(chunks)
    masked = bias is not None
    kernel = functools.partial(
        stage_kernel,
        n_chunks=n_chunks,
        first=first,
        last=last,
        masked=masked,
        scale=HEAD_DIM ** (-0.5),
    )
    row_spec = pl.BlockSpec((rows, HEAD_DIM), lambda h: (row_block, h))
    in_specs = []
    operands = []
    if masked:
        in_specs.append(pl.BlockSpec(bias.shape, lambda h: (0, 0)))
        operands.append(bias)
    in_specs.append(row_spec)
    operands.append(queries)
    for chunk in chunks:
        width = chunk.shape[0]
        in_specs.append(pl.BlockSpec((width, HEAD_DIM), lambda h: (0, h)))
        in_specs.append(pl.BlockSpec((width, HEAD_DIM), lambda h: (0, heads + h)))
        operands += [chunk, chunk]
    if not first:
        in_specs += [row_spec] * 3
        operands += list(carry)
    out_spec = pl.BlockSpec((rows, HEAD_DIM), lambda h: (0, h))
    if last:
        out_shape = jax.ShapeDtypeStruct((rows, heads * HEAD_DIM), jnp.bfloat16)
        out_specs = out_spec
    else:
        out_shape = [jax.ShapeDtypeStruct((rows, heads * HEAD_DIM), jnp.float32)] * 3
        out_specs = [out_spec] * 3
    return pl.pallas_call(
        kernel,
        out_shape=out_shape,
        grid=(heads,),
        in_specs=in_specs,
        out_specs=out_specs,
        compiler_params=pltpu.CompilerParams(dimension_semantics=("arbitrary",)),
    )(*operands)


def per_device_body(tokens, modulation, w_qkv, w_out, adjacency):
    inputs = tokens[0, 0].astype(jnp.float32)
    width = inputs.shape[1]
    half_heads = w_qkv.shape[2]
    heads = half_heads // HEAD_DIM
    shift_scale = modulation[0]
    squares = jnp.mean(inputs * inputs, axis=1, keepdims=True)
    normed = (inputs * lax.rsqrt(squares + 1e-06) * (1.0 + shift_scale[1]) + shift_scale[0]).astype(
        jnp.bfloat16
    )
    half_rows = normed.shape[0]
    partner_normed = swap(normed, "tp")
    kv_w = w_qkv[:, 1:, :].reshape(width, 2 * half_heads)
    q_w = w_qkv[:, 0, :]
    pair_own = jnp.dot(normed, kv_w, preferred_element_type=jnp.float32).astype(jnp.bfloat16)

    near_own = {sign: from_behind(pair_own, "orbit", -sign) for sign in (1, -1)}

    pair_other = jnp.dot(partner_normed, kv_w, preferred_element_type=jnp.float32).astype(
        jnp.bfloat16
    )
    both_rows = jnp.concatenate([normed, partner_normed], axis=0)
    queries = jnp.dot(both_rows, q_w, preferred_element_type=jnp.float32).astype(jnp.bfloat16)

    tp_index = lax.axis_index("tp")
    flags = adjacency[0]
    blocks = flags.shape[1]
    per_chunk = blocks // 2
    own_start = tp_index * per_chunk
    other_start = (1 - tp_index) * per_chunk

    def chunk_bias(offsets, start, count):
        rows_of = []
        for offset in offsets:
            row = flags[offset + REACH if offset < 0 else offset + REACH - 1]
            rows_of.append(lax.dynamic_slice_in_dim(row, start, count))
        allowed = jnp.repeat(jnp.concatenate(rows_of), BLOCK) > 0
        return jnp.where(allowed, 0.0, -1e30).astype(jnp.float32)[None, :]

    carry = attend_stage(
        queries, [pair_own, pair_other], None, None, first=True, last=False, heads=heads
    )
    pair_other, carry = lax.optimization_barrier((pair_other, carry))
    piece_rows = half_rows // 2
    piece_blocks = per_chunk // 2
    other_pieces = [pair_other[:piece_rows], pair_other[piece_rows:]]
    near_other = {
        sign: [from_behind(piece, "orbit", -sign) for piece in other_pieces] for sign in (1, -1)
    }
    far_own = {sign: from_behind(near_own[sign], "orbit", -sign) for sign in (1, -1)}
    carry = attend_stage(
        queries, [near_own[-1], near_own[1]], chunk_bias((-1, 1), own_start, per_chunk), carry,
        first=False, last=False, heads=heads,
    )
    far_other = {
        sign: [from_behind(piece, "orbit", -sign) for piece in near_other[sign]] for sign in (1, -1)
    }
    near_bias = jnp.concatenate(
        [chunk_bias((-1, 1), other_start + k * piece_blocks, piece_blocks) for k in range(2)],
        axis=1,
    )
    carry = attend_stage(
        queries,
        [near_other[-1][0], near_other[1][0], near_other[-1][1], near_other[1][1]],
        near_bias, carry, first=False, last=False, heads=heads,
    )
    carry = attend_stage(
        queries, [far_own[-1], far_own[1]], chunk_bias((-2, 2), own_start, per_chunk), carry,
        first=False, last=False, heads=heads,
    )
    carry = attend_stage(
        queries, [far_other[-1][0], far_other[1][0]],
        chunk_bias((-2, 2), other_start, piece_blocks), carry,
        first=False, last=False, heads=heads,
    )
    last_chunks = [far_other[-1][1], far_other[1][1]]
    last_bias = chunk_bias((-2, 2), other_start + piece_blocks, piece_blocks)
    context_other = attend_stage(
        queries, last_chunks, last_bias, carry,
        first=False, last=True, heads=heads, row_block=1, rows=half_rows,
    )

    owner = lax.axis_index("cfg")
    half_width = width // 2
    weight_now = jnp.where(owner == 0, guide_scale, 1.0 - guide_scale).astype(jnp.float32)
    w_mine = lax.dynamic_slice_in_dim(w_out, owner * half_width, half_width, 1)
    w_theirs = lax.dynamic_slice_in_dim(w_out, (1 - owner) * half_width, half_width, 1)

    def project(context):
        theirs = weight_now * jnp.dot(context, w_theirs, preferred_element_type=jnp.float32)
        mine = weight_now * jnp.dot(context, w_mine, preferred_element_type=jnp.float32)
        return mine + swap(theirs, "cfg")

    to_partner = project(context_other).astype(jnp.bfloat16)
    to_partner, carry = lax.optimization_barrier((to_partner, carry))
    from_partner = swap(to_partner, "tp")
    context_own = attend_stage(
        queries, last_chunks, last_bias, carry,
        first=False, last=True, heads=heads, row_block=0, rows=half_rows,
    )
    guided = project(context_own) + from_partner.astype(jnp.float32)
    return guided.astype(jnp.bfloat16)[None]


def solution(mesh):
    return jax.shard_map(
        per_device_body,
        mesh=mesh,
        in_specs=(
            P("cfg", "orbit", "tp", None),
            P("cfg", None, None),
            P(None, None, "tp"),
            P("tp", None),
            P("orbit", None, None),
        ),
        out_specs=P("orbit", "tp", "cfg"),
        check_vma=False,
    )
```

```python
import functools

import jax
import jax.numpy as jnp
from jax import lax
from jax.experimental import pallas as pl
from jax.experimental.pallas import tpu as pltpu
from jax.sharding import PartitionSpec as P


HEAD_DIM = 128
REACH = 2
BLOCK = 128


guide_scale = 4.0


def from_behind(array, axis, by):
    count = lax.axis_size(axis)
    return lax.ppermute(array, axis, [(i, (i + by) % count) for i in range(count)])


def swap(array, axis):
    return lax.ppermute(array, axis, [(0, 1), (1, 0)])


def stage_kernel(*refs, n_chunks, first, last, masked, scale):
    refs = list(refs)
    bias_ref = refs.pop(0) if masked else None
    q_ref = refs.pop(0)
    chunk_refs = refs[: 2 * n_chunks]
    rest = refs[2 * n_chunks :]
    if first:
        outs = rest
    else:
        m_in, l_in, acc_in = rest[:3]
        outs = rest[3:]
    q = q_ref[...]
    rows = q.shape[0]
    if first:
        m = jnp.full((rows, HEAD_DIM), -jnp.inf, jnp.float32)
        l = jnp.zeros((rows, HEAD_DIM), jnp.float32)
        acc = jnp.zeros((rows, HEAD_DIM), jnp.float32)
    else:
        m = m_in[...]
        l = l_in[...]
        acc = acc_in[...]
    for index in range(n_chunks):
        keys = chunk_refs[2 * index][...]
        values = chunk_refs[2 * index + 1][...]
        width = keys.shape[0]
        scores = lax.dot_general(
            q, keys, (((1,), (1,)), ((), ())), preferred_element_type=jnp.float32
        ) * scale
        if masked:
            scores = scores + bias_ref[:, index * width : (index + 1) * width]
        m_new = jnp.maximum(m, jnp.max(scores, axis=1, keepdims=True))
        alpha = jnp.exp(m - m_new)
        expon = jnp.exp(scores - jnp.tile(m_new, (1, width // HEAD_DIM)))
        l = alpha * l + jnp.sum(expon, axis=1, keepdims=True)
        acc = alpha * acc + jnp.dot(
            expon.astype(jnp.bfloat16), values, preferred_element_type=jnp.float32
        )
        m = m_new
    if last:
        outs[0][...] = (acc / l).astype(outs[0].dtype)
    else:
        outs[0][...] = m
        outs[1][...] = l
        outs[2][...] = acc


def attend_stage(queries, chunks, bias, carry, *, first, last, heads, row_block=0, rows=None):
    rows = queries.shape[0] if rows is None else rows
    n_chunks = len(chunks)
    masked = bias is not None
    kernel = functools.partial(
        stage_kernel,
        n_chunks=n_chunks,
        first=first,
        last=last,
        masked=masked,
        scale=HEAD_DIM ** (-0.5),
    )
    row_spec = pl.BlockSpec((rows, HEAD_DIM), lambda h: (row_block, h))
    in_specs = []
    operands = []
    if masked:
        in_specs.append(pl.BlockSpec(bias.shape, lambda h: (0, 0)))
        operands.append(bias)
    in_specs.append(row_spec)
    operands.append(queries)
    for chunk in chunks:
        width = chunk.shape[0]
        in_specs.append(pl.BlockSpec((width, HEAD_DIM), lambda h: (0, h)))
        in_specs.append(pl.BlockSpec((width, HEAD_DIM), lambda h: (0, heads + h)))
        operands += [chunk, chunk]
    if not first:
        in_specs += [row_spec] * 3
        operands += list(carry)
    out_spec = pl.BlockSpec((rows, HEAD_DIM), lambda h: (0, h))
    if last:
        out_shape = jax.ShapeDtypeStruct((rows, heads * HEAD_DIM), jnp.bfloat16)
        out_specs = out_spec
    else:
        out_shape = [jax.ShapeDtypeStruct((rows, heads * HEAD_DIM), jnp.float32)] * 3
        out_specs = [out_spec] * 3
    return pl.pallas_call(
        kernel,
        out_shape=out_shape,
        grid=(heads,),
        in_specs=in_specs,
        out_specs=out_specs,
        compiler_params=pltpu.CompilerParams(dimension_semantics=("arbitrary",)),
    )(*operands)


def per_device_body(tokens, modulation, w_qkv, w_out, adjacency):
    inputs = tokens[0, 0].astype(jnp.float32)
    width = inputs.shape[1]
    half_heads = w_qkv.shape[2]
    heads = half_heads // HEAD_DIM
    shift_scale = modulation[0]
    squares = jnp.mean(inputs * inputs, axis=1, keepdims=True)
    normed = (inputs * lax.rsqrt(squares + 1e-06) * (1.0 + shift_scale[1]) + shift_scale[0]).astype(
        jnp.bfloat16
    )
    half_rows = normed.shape[0]
    partner_normed = swap(normed, "tp")
    kv_w = w_qkv[:, 1:, :].reshape(width, 2 * half_heads)
    q_w = w_qkv[:, 0, :]
    pair_own = jnp.dot(normed, kv_w, preferred_element_type=jnp.float32).astype(jnp.bfloat16)

    near_own = {sign: from_behind(pair_own, "orbit", -sign) for sign in (1, -1)}

    pair_other = jnp.dot(partner_normed, kv_w, preferred_element_type=jnp.float32).astype(
        jnp.bfloat16
    )
    both_rows = jnp.concatenate([normed, partner_normed], axis=0)
    queries = jnp.dot(both_rows, q_w, preferred_element_type=jnp.float32).astype(jnp.bfloat16)

    tp_index = lax.axis_index("tp")
    flags = adjacency[0]
    blocks = flags.shape[1]
    per_chunk = blocks // 2
    own_start = tp_index * per_chunk
    other_start = (1 - tp_index) * per_chunk

    def chunk_bias(offsets, start):
        rows_of = []
        for offset in offsets:
            row = flags[offset + REACH if offset < 0 else offset + REACH - 1]
            rows_of.append(lax.dynamic_slice_in_dim(row, start, per_chunk))
        allowed = jnp.repeat(jnp.concatenate(rows_of), BLOCK) > 0
        return jnp.where(allowed, 0.0, -1e30).astype(jnp.float32)[None, :]

    carry = attend_stage(
        queries, [pair_own, pair_other], None, None, first=True, last=False, heads=heads
    )
    pair_other, carry = lax.optimization_barrier((pair_other, carry))
    near_other = {sign: from_behind(pair_other, "orbit", -sign) for sign in (1, -1)}
    far_own = {sign: from_behind(near_own[sign], "orbit", -sign) for sign in (1, -1)}
    carry = attend_stage(
        queries, [near_own[-1], near_own[1]], chunk_bias((-1, 1), own_start), carry,
        first=False, last=False, heads=heads,
    )
    far_other = {sign: from_behind(near_other[sign], "orbit", -sign) for sign in (1, -1)}
    carry = attend_stage(
        queries, [near_other[-1], near_other[1]], chunk_bias((-1, 1), other_start), carry,
        first=False, last=False, heads=heads,
    )
    carry = attend_stage(
        queries, [far_own[-1], far_own[1]], chunk_bias((-2, 2), own_start), carry,
        first=False, last=False, heads=heads,
    )
    last_chunks = [far_other[-1], far_other[1]]
    last_bias = chunk_bias((-2, 2), other_start)
    context_other = attend_stage(
        queries, last_chunks, last_bias, carry,
        first=False, last=True, heads=heads, row_block=1, rows=half_rows,
    )
    owner = lax.axis_index("cfg")
    half_width = width // 2
    weight_now = jnp.where(owner == 0, guide_scale, 1.0 - guide_scale).astype(jnp.float32)
    weight_other = jnp.where(owner == 0, 1.0 - guide_scale, guide_scale).astype(jnp.float32)
    w_mine = lax.dynamic_slice_in_dim(w_out, owner * half_width, half_width, 1)

    def project(context):
        other_branch = swap(context, "cfg")
        mine = weight_now * jnp.dot(context, w_mine, preferred_element_type=jnp.float32)
        return mine + weight_other * jnp.dot(
            other_branch, w_mine, preferred_element_type=jnp.float32
        )

    to_partner = project(context_other).astype(jnp.bfloat16)
    to_partner, carry = lax.optimization_barrier((to_partner, carry))
    from_partner = swap(to_partner, "tp")
    context_own = attend_stage(
        queries, last_chunks, last_bias, carry,
        first=False, last=True, heads=heads, row_block=0, rows=half_rows,
    )
    guided = project(context_own) + from_partner.astype(jnp.float32)
    return guided.astype(jnp.bfloat16)[None]


def solution(mesh):
    return jax.shard_map(
        per_device_body,
        mesh=mesh,
        in_specs=(
            P("cfg", "orbit", "tp", None),
            P("cfg", None, None),
            P(None, None, "tp"),
            P("tp", None),
            P("orbit", None, None),
        ),
        out_specs=P("orbit", "tp", "cfg"),
        check_vma=False,
    )
```

```python
import functools

import jax
import jax.numpy as jnp
from jax import lax
from jax.experimental import pallas as pl
from jax.experimental.pallas import tpu as pltpu
from jax.sharding import PartitionSpec as P


HEAD_DIM = 128
REACH = 2
BLOCK = 128


guide_scale = 4.0


def from_behind(array, axis, by):
    count = lax.axis_size(axis)
    return lax.ppermute(array, axis, [(i, (i + by) % count) for i in range(count)])


def swap(array, axis):
    return lax.ppermute(array, axis, [(0, 1), (1, 0)])


def stage_kernel(*refs, n_chunks, first, last, masked, scale):
    refs = list(refs)
    bias_ref = refs.pop(0) if masked else None
    q_ref = refs.pop(0)
    chunk_refs = refs[: 2 * n_chunks]
    rest = refs[2 * n_chunks :]
    if first:
        outs = rest
    else:
        m_in, l_in, acc_in = rest[:3]
        outs = rest[3:]
    q = q_ref[...]
    rows = q.shape[0]
    if first:
        m = jnp.full((rows, HEAD_DIM), -jnp.inf, jnp.float32)
        l = jnp.zeros((rows, HEAD_DIM), jnp.float32)
        acc = jnp.zeros((rows, HEAD_DIM), jnp.float32)
    else:
        m = m_in[...]
        l = l_in[...]
        acc = acc_in[...]
    for index in range(n_chunks):
        keys = chunk_refs[2 * index][...]
        values = chunk_refs[2 * index + 1][...]
        width = keys.shape[0]
        scores = lax.dot_general(
            q, keys, (((1,), (1,)), ((), ())), preferred_element_type=jnp.float32
        ) * scale
        if masked:
            scores = scores + bias_ref[:, index * width : (index + 1) * width]
        m_new = jnp.maximum(m, jnp.max(scores, axis=1, keepdims=True))
        alpha = jnp.exp(m - m_new)
        expon = jnp.exp(scores - jnp.tile(m_new, (1, width // HEAD_DIM)))
        l = alpha * l + jnp.sum(expon, axis=1, keepdims=True)
        acc = alpha * acc + jnp.dot(
            expon.astype(jnp.bfloat16), values, preferred_element_type=jnp.float32
        )
        m = m_new
    if last:
        outs[0][...] = (acc / l).astype(outs[0].dtype)
    else:
        outs[0][...] = m
        outs[1][...] = l
        outs[2][...] = acc


def attend_stage(queries, chunks, bias, carry, *, first, last, heads, row_block=0, rows=None):
    rows = queries.shape[0] if rows is None else rows
    n_chunks = len(chunks)
    masked = bias is not None
    kernel = functools.partial(
        stage_kernel,
        n_chunks=n_chunks,
        first=first,
        last=last,
        masked=masked,
        scale=HEAD_DIM ** (-0.5),
    )
    row_spec = pl.BlockSpec((rows, HEAD_DIM), lambda h: (row_block, h))
    in_specs = []
    operands = []
    if masked:
        in_specs.append(pl.BlockSpec(bias.shape, lambda h: (0, 0)))
        operands.append(bias)
    in_specs.append(row_spec)
    operands.append(queries)
    for chunk in chunks:
        width = chunk.shape[0]
        in_specs.append(pl.BlockSpec((width, HEAD_DIM), lambda h: (0, h)))
        in_specs.append(pl.BlockSpec((width, HEAD_DIM), lambda h: (0, heads + h)))
        operands += [chunk, chunk]
    if not first:
        in_specs += [row_spec] * 3
        operands += list(carry)
    out_spec = pl.BlockSpec((rows, HEAD_DIM), lambda h: (0, h))
    if last:
        out_shape = jax.ShapeDtypeStruct((rows, heads * HEAD_DIM), jnp.bfloat16)
        out_specs = out_spec
    else:
        out_shape = [jax.ShapeDtypeStruct((rows, heads * HEAD_DIM), jnp.float32)] * 3
        out_specs = [out_spec] * 3
    return pl.pallas_call(
        kernel,
        out_shape=out_shape,
        grid=(heads,),
        in_specs=in_specs,
        out_specs=out_specs,
        compiler_params=pltpu.CompilerParams(dimension_semantics=("arbitrary",)),
    )(*operands)


def per_device_body(tokens, modulation, w_qkv, w_out, adjacency):
    inputs = tokens[0, 0].astype(jnp.float32)
    width = inputs.shape[1]
    half_heads = w_qkv.shape[2]
    heads = half_heads // HEAD_DIM
    shift_scale = modulation[0]
    squares = jnp.mean(inputs * inputs, axis=1, keepdims=True)
    normed = (inputs * lax.rsqrt(squares + 1e-06) * (1.0 + shift_scale[1]) + shift_scale[0]).astype(
        jnp.bfloat16
    )
    half_rows = normed.shape[0]
    partner_normed = swap(normed, "tp")
    kv_w = w_qkv[:, 1:, :].reshape(width, 2 * half_heads)
    q_w = w_qkv[:, 0, :]
    pair_own = jnp.einsum(
        "rk,kjn->rjn", normed, w_qkv[:, 1:, :], preferred_element_type=jnp.float32
    ).astype(jnp.bfloat16).reshape(half_rows, 2 * half_heads)

    near_own = {sign: from_behind(pair_own, "orbit", -sign) for sign in (1, -1)}

    pair_other = jnp.dot(partner_normed, kv_w, preferred_element_type=jnp.float32).astype(
        jnp.bfloat16
    )
    both_rows = jnp.concatenate([normed, partner_normed], axis=0)
    queries = jnp.dot(both_rows, q_w, preferred_element_type=jnp.float32).astype(jnp.bfloat16)

    tp_index = lax.axis_index("tp")
    flags = adjacency[0]
    blocks = flags.shape[1]
    per_chunk = blocks // 2
    own_start = tp_index * per_chunk
    other_start = (1 - tp_index) * per_chunk

    def chunk_bias(offsets, start):
        rows_of = []
        for offset in offsets:
            row = flags[offset + REACH if offset < 0 else offset + REACH - 1]
            rows_of.append(lax.dynamic_slice_in_dim(row, start, per_chunk))
        allowed = jnp.repeat(jnp.concatenate(rows_of), BLOCK) > 0
        return jnp.where(allowed, 0.0, -1e30).astype(jnp.float32)[None, :]

    carry = attend_stage(
        queries, [pair_own, pair_other], None, None, first=True, last=False, heads=heads
    )
    near_other = {sign: from_behind(pair_other, "orbit", -sign) for sign in (1, -1)}
    far_own = {sign: from_behind(near_own[sign], "orbit", -sign) for sign in (1, -1)}
    carry = attend_stage(
        queries, [near_own[-1], near_own[1]], chunk_bias((-1, 1), own_start), carry,
        first=False, last=False, heads=heads,
    )
    far_other = {sign: from_behind(near_other[sign], "orbit", -sign) for sign in (1, -1)}
    carry = attend_stage(
        queries, [near_other[-1], near_other[1]], chunk_bias((-1, 1), other_start), carry,
        first=False, last=False, heads=heads,
    )
    carry = attend_stage(
        queries, [far_own[-1], far_own[1]], chunk_bias((-2, 2), own_start), carry,
        first=False, last=False, heads=heads,
    )
    last_chunks = [far_other[-1], far_other[1]]
    last_bias = chunk_bias((-2, 2), other_start)
    context_other = attend_stage(
        queries, last_chunks, last_bias, carry,
        first=False, last=True, heads=heads, row_block=1, rows=half_rows,
    )
    owner = lax.axis_index("cfg")
    half_width = width // 2
    weight_now = jnp.where(owner == 0, guide_scale, 1.0 - guide_scale).astype(jnp.float32)
    weight_other = jnp.where(owner == 0, 1.0 - guide_scale, guide_scale).astype(jnp.float32)
    w_mine = lax.dynamic_slice_in_dim(w_out, owner * half_width, half_width, 1)

    def project(context):
        other_branch = swap(context, "cfg")
        mine = weight_now * jnp.dot(context, w_mine, preferred_element_type=jnp.float32)
        return mine + weight_other * jnp.dot(
            other_branch, w_mine, preferred_element_type=jnp.float32
        )

    to_partner = project(context_other).astype(jnp.bfloat16)
    to_partner, carry = lax.optimization_barrier((to_partner, carry))
    from_partner = swap(to_partner, "tp")
    context_own = attend_stage(
        queries, last_chunks, last_bias, carry,
        first=False, last=True, heads=heads, row_block=0, rows=half_rows,
    )
    guided = project(context_own) + from_partner.astype(jnp.float32)
    return guided.astype(jnp.bfloat16)[None]


def solution(mesh):
    return jax.shard_map(
        per_device_body,
        mesh=mesh,
        in_specs=(
            P("cfg", "orbit", "tp", None),
            P("cfg", None, None),
            P(None, None, "tp"),
            P("tp", None),
            P("orbit", None, None),
        ),
        out_specs=P("orbit", "tp", "cfg"),
        check_vma=False,
    )
```

```python
import functools

import jax
import jax.numpy as jnp
from jax import lax
from jax.experimental import pallas as pl
from jax.experimental.pallas import tpu as pltpu
from jax.sharding import PartitionSpec as P


HEAD_DIM = 128
REACH = 2
BLOCK = 128


guide_scale = 4.0


def from_behind(array, axis, by):
    count = lax.axis_size(axis)
    return lax.ppermute(array, axis, [(i, (i + by) % count) for i in range(count)])


def swap(array, axis):
    return lax.ppermute(array, axis, [(0, 1), (1, 0)])


def stage_kernel(*refs, n_chunks, first, last, masked, scale):
    refs = list(refs)
    bias_ref = refs.pop(0) if masked else None
    q_ref = refs.pop(0)
    chunk_refs = refs[: 2 * n_chunks]
    rest = refs[2 * n_chunks :]
    if first:
        outs = rest
    else:
        m_in, l_in, acc_in = rest[:3]
        outs = rest[3:]
    q = q_ref[...]
    rows = q.shape[0]
    if first:
        m = jnp.full((rows, HEAD_DIM), -jnp.inf, jnp.float32)
        l = jnp.zeros((rows, HEAD_DIM), jnp.float32)
        acc = jnp.zeros((rows, HEAD_DIM), jnp.float32)
    else:
        m = m_in[...]
        l = l_in[...]
        acc = acc_in[...]
    for index in range(n_chunks):
        keys = chunk_refs[2 * index][...]
        values = chunk_refs[2 * index + 1][...]
        width = keys.shape[0]
        scores = lax.dot_general(
            q, keys, (((1,), (1,)), ((), ())), preferred_element_type=jnp.float32
        ) * scale
        if masked:
            scores = scores + bias_ref[:, index * width : (index + 1) * width]
        m_new = jnp.maximum(m, jnp.max(scores, axis=1, keepdims=True))
        alpha = jnp.exp2(m - m_new)
        expon = jnp.exp2(scores - jnp.tile(m_new, (1, width // HEAD_DIM)))
        l = alpha * l + jnp.sum(expon, axis=1, keepdims=True)
        acc = alpha * acc + jnp.dot(
            expon.astype(jnp.bfloat16), values, preferred_element_type=jnp.float32
        )
        m = m_new
    if last:
        outs[0][...] = (acc / l).astype(outs[0].dtype)
    else:
        outs[0][...] = m
        outs[1][...] = l
        outs[2][...] = acc


def attend_stage(queries, chunks, bias, carry, *, first, last, heads, row_block=0, rows=None):
    rows = queries.shape[0] if rows is None else rows
    n_chunks = len(chunks)
    masked = bias is not None
    kernel = functools.partial(
        stage_kernel,
        n_chunks=n_chunks,
        first=first,
        last=last,
        masked=masked,
        scale=HEAD_DIM ** (-0.5) * 1.4426950408889634,
    )
    row_spec = pl.BlockSpec((rows, HEAD_DIM), lambda h: (row_block, h))
    in_specs = []
    operands = []
    if masked:
        in_specs.append(pl.BlockSpec(bias.shape, lambda h: (0, 0)))
        operands.append(bias)
    in_specs.append(row_spec)
    operands.append(queries)
    for chunk in chunks:
        width = chunk.shape[0]
        in_specs.append(pl.BlockSpec((width, HEAD_DIM), lambda h: (0, h)))
        in_specs.append(pl.BlockSpec((width, HEAD_DIM), lambda h: (0, heads + h)))
        operands += [chunk, chunk]
    if not first:
        in_specs += [row_spec] * 3
        operands += list(carry)
    out_spec = pl.BlockSpec((rows, HEAD_DIM), lambda h: (0, h))
    if last:
        out_shape = jax.ShapeDtypeStruct((rows, heads * HEAD_DIM), jnp.bfloat16)
        out_specs = out_spec
    else:
        out_shape = [jax.ShapeDtypeStruct((rows, heads * HEAD_DIM), jnp.float32)] * 3
        out_specs = [out_spec] * 3
    return pl.pallas_call(
        kernel,
        out_shape=out_shape,
        grid=(heads,),
        in_specs=in_specs,
        out_specs=out_specs,
        compiler_params=pltpu.CompilerParams(dimension_semantics=("arbitrary",)),
    )(*operands)


def per_device_body(tokens, modulation, w_qkv, w_out, adjacency):
    inputs = tokens[0, 0].astype(jnp.float32)
    width = inputs.shape[1]
    half_heads = w_qkv.shape[2]
    heads = half_heads // HEAD_DIM
    shift_scale = modulation[0]
    squares = jnp.mean(inputs * inputs, axis=1, keepdims=True)
    normed = (inputs * lax.rsqrt(squares + 1e-06) * (1.0 + shift_scale[1]) + shift_scale[0]).astype(
        jnp.bfloat16
    )
    half_rows = normed.shape[0]
    partner_normed = swap(normed, "tp")
    kv_w = w_qkv[:, 1:, :].reshape(width, 2 * half_heads)
    q_w = w_qkv[:, 0, :]
    pair_own = jnp.dot(normed, kv_w, preferred_element_type=jnp.float32).astype(jnp.bfloat16)

    near_own = {sign: from_behind(pair_own, "orbit", -sign) for sign in (1, -1)}

    pair_other = jnp.dot(partner_normed, kv_w, preferred_element_type=jnp.float32).astype(
        jnp.bfloat16
    )
    both_rows = jnp.concatenate([normed, partner_normed], axis=0)
    queries = jnp.dot(both_rows, q_w, preferred_element_type=jnp.float32).astype(jnp.bfloat16)

    tp_index = lax.axis_index("tp")
    flags = adjacency[0]
    blocks = flags.shape[1]
    per_chunk = blocks // 2
    own_start = tp_index * per_chunk
    other_start = (1 - tp_index) * per_chunk

    def chunk_bias(offsets, start):
        rows_of = []
        for offset in offsets:
            row = flags[offset + REACH if offset < 0 else offset + REACH - 1]
            rows_of.append(lax.dynamic_slice_in_dim(row, start, per_chunk))
        allowed = jnp.repeat(jnp.concatenate(rows_of), BLOCK) > 0
        return jnp.where(allowed, 0.0, -1e30).astype(jnp.float32)[None, :]

    carry = attend_stage(
        queries, [pair_own, pair_other], None, None, first=True, last=False, heads=heads
    )
    pair_other, carry = lax.optimization_barrier((pair_other, carry))
    near_other = {sign: from_behind(pair_other, "orbit", -sign) for sign in (1, -1)}
    far_own = {sign: from_behind(near_own[sign], "orbit", -sign) for sign in (1, -1)}
    carry = attend_stage(
        queries, [near_own[-1], near_own[1]], chunk_bias((-1, 1), own_start), carry,
        first=False, last=False, heads=heads,
    )
    far_other = {sign: from_behind(near_other[sign], "orbit", -sign) for sign in (1, -1)}
    carry = attend_stage(
        queries, [near_other[-1], near_other[1]], chunk_bias((-1, 1), other_start), carry,
        first=False, last=False, heads=heads,
    )
    carry = attend_stage(
        queries, [far_own[-1], far_own[1]], chunk_bias((-2, 2), own_start), carry,
        first=False, last=False, heads=heads,
    )
    last_chunks = [far_other[-1], far_other[1]]
    last_bias = chunk_bias((-2, 2), other_start)
    context_other = attend_stage(
        queries, last_chunks, last_bias, carry,
        first=False, last=True, heads=heads, row_block=1, rows=half_rows,
    )
    owner = lax.axis_index("cfg")
    half_width = width // 2
    weight_now = jnp.where(owner == 0, guide_scale, 1.0 - guide_scale).astype(jnp.float32)
    weight_other = jnp.where(owner == 0, 1.0 - guide_scale, guide_scale).astype(jnp.float32)
    w_mine = lax.dynamic_slice_in_dim(w_out, owner * half_width, half_width, 1)

    def project(context):
        other_branch = swap(context, "cfg")
        mine = weight_now * jnp.dot(context, w_mine, preferred_element_type=jnp.float32)
        return mine + weight_other * jnp.dot(
            other_branch, w_mine, preferred_element_type=jnp.float32
        )

    to_partner = project(context_other).astype(jnp.bfloat16)
    to_partner, carry = lax.optimization_barrier((to_partner, carry))
    from_partner = swap(to_partner, "tp")
    context_own = attend_stage(
        queries, last_chunks, last_bias, carry,
        first=False, last=True, heads=heads, row_block=0, rows=half_rows,
    )
    guided = project(context_own) + from_partner.astype(jnp.float32)
    return guided.astype(jnp.bfloat16)[None]


def solution(mesh):
    return jax.shard_map(
        per_device_body,
        mesh=mesh,
        in_specs=(
            P("cfg", "orbit", "tp", None),
            P("cfg", None, None),
            P(None, None, "tp"),
            P("tp", None),
            P("orbit", None, None),
        ),
        out_specs=P("orbit", "tp", "cfg"),
        check_vma=False,
    )
```
